256 devices in a mesh: up: 32 (over y, z), down: 8 (over x, core).
Axes of the slice: x: 4, y: 4, z: 8, core: 2. Of those that a mesh axis runs over, the one named last changes fastest.
Arguments:
- amplitudes: float32 [4096, 4096], P('up', 'down'), may hold values from -6 to 6
- double_occ: int32 [4096, 4096], P('up', 'down'), may hold values from 0 to 8
- up_cols: int32 [64, 32], replicated, may hold values from 0 to 63, as said below
- up_ids: int32 [64, 32], replicated, may hold values from 0 to 31, as said below
- up_blocks: bfloat16 [32, 64, 64], replicated, may hold values from -0.125 to 0.125
- down_cols: int32 [64, 32], replicated, may hold values from 0 to 63, as said below
- down_ids: int32 [64, 32], replicated, may hold values from 0 to 31, as said below
- down_blocks: bfloat16 [32, 64, 64], replicated, may hold values from -0.125 to 0.125
Outputs:
- chebyshev: float32 [4096, 4096], P('up', 'down')
The draws below stay inside these ranges and needn't reach their ends.
Inputs may be any that keep to these rules, and one draw needn't show every extreme that they name: `up_cols`: each row names 32 different blocks. `up_ids`: each row names every shared block exactly once. `down_cols`: each row names 32 different blocks. `down_ids`: each row names every shared block exactly once.
All inputs are finite; a program needn't handle non-finite values.
Results may differ from the reference program's by a relative error of at most 0.0031.
Values may be sent and summed in bfloat16 or wider, within the bound.
No kernel may reach another device: no remote copies, remote signals or barrier semaphores. Data moves between devices by JAX's collectives and lax.ppermute only.
A program may use at most 64 MiB of HBM per device.

```python
import jax
import jax.numpy as jnp
from jax import lax

BLK = 64
NBLK = 64
BPR = 32
NSTR = 4096


def pattern_cols(key):

    def one_row(row_key):
        return jax.random.permutation(row_key, NBLK).astype(jnp.int32)
    orders = jax.vmap(one_row)(jax.random.split(key, NBLK))
    rank_table = jnp.argsort(orders, axis=1, stable=True).astype(jnp.int32)
    blocks_all = jnp.arange(NBLK, dtype=jnp.int32)
    end_blocks = (blocks_all == 0) | (blocks_all == NBLK - 1)
    scores = jnp.where(end_blocks, -1, rank_table[0])
    chosen = jnp.argsort(scores, stable=True).astype(jnp.int32)[:BPR]
    return orders[:, :BPR].at[0].set(chosen).astype(jnp.int32)


def pattern_ids(key):

    def one_row(row_key):
        return jax.random.permutation(row_key, BPR).astype(jnp.int32)
    return jax.vmap(one_row)(jax.random.split(key, NBLK)).astype(jnp.int32)


def draw_up_cols(key, part):
    return pattern_cols(jax.random.fold_in(key, 11))


def draw_down_cols(key, part):
    return pattern_cols(jax.random.fold_in(key, 23))


def draw_up_ids(key, part):
    return pattern_ids(jax.random.fold_in(key, 31))


def draw_down_ids(key, part):
    return pattern_ids(jax.random.fold_in(key, 47))


def plant(entries, own_key, least, high):
    extent = entries.shape
    place = [jax.random.randint(jax.random.fold_in(own_key, axis), (), 0, extent[axis]) for axis in range(len(extent))]
    entries = entries.at[tuple(place)].set(least)
    longest = extent.index(max(extent))
    place[longest] = (place[longest] + 1) % extent[longest]
    return entries.at[tuple(place)].set(high)


def levels(own_key, dims, cuts, low, largest):
    loudness, own = 1.0, jax.random.fold_in(own_key, 6)
    for position, parts in cuts:
        steps = jnp.exp(jax.random.uniform(jax.random.fold_in(own, position), (parts,), jnp.float32, low / len(cuts), largest / len(cuts)))
        loudness = loudness * jnp.repeat(steps, dims[position] // parts).reshape([-1 if axis == position else 1 for axis in range(len(dims))])
    return loudness


def bell_draw(key, dims, width, reach, cuts=(), kind=jnp.bfloat16):
    loudness = levels(key, dims, cuts, -0.22, 0.18) if cuts else 1.0
    entries = jax.random.normal(key, dims, jnp.float32) * width * loudness
    return jnp.minimum(jnp.maximum(entries, -reach), reach).astype(kind)


def setup_inputs(seed: int = 0) -> dict:
    keys = jax.random.split(jax.random.key(seed), 9)
    amplitudes = bell_draw(keys[0], (NSTR, NSTR), 1.0, 6.0, ((0, 32), (1, 8)), jnp.float32)
    double_occ = plant(jax.random.randint(keys[1], (NSTR, NSTR), 0, 9), jax.random.fold_in(keys[1], 1), 0, 8).astype(jnp.int32)
    up_cols = draw_up_cols(jax.random.fold_in(keys[8], 71), 0)
    up_ids = draw_up_ids(jax.random.fold_in(keys[8], 71), 0)
    up_blocks = bell_draw(keys[4], (BPR, BLK, BLK), (BPR * BLK) ** -0.5, 0.125)
    down_cols = draw_down_cols(jax.random.fold_in(keys[8], 71), 0)
    down_ids = draw_down_ids(jax.random.fold_in(keys[8], 71), 0)
    down_blocks = bell_draw(keys[7], (BPR, BLK, BLK), (BPR * BLK) ** -0.5, 0.125)
    return dict(amplitudes=amplitudes, double_occ=double_occ, up_cols=up_cols, up_ids=up_ids, up_blocks=up_blocks, down_cols=down_cols, down_ids=down_ids, down_blocks=down_blocks)


coupling = 0.5
center = 2.0
half_span = 2.0


def hop_last(values, block_cols, block_ids, shared_table):
    row_count = values.shape[0]
    block_width = shared_table.shape[1]
    block_total = values.shape[1] // block_width
    pieces = values.astype(jnp.float32).reshape(row_count, block_total, block_width)
    wide_table = shared_table.astype(jnp.float32)

    def one_block(row_pattern):
        row_cols, row_ids = row_pattern
        taken_rows = jnp.take(pieces, row_cols.astype(jnp.int32), axis=1)
        weights = jnp.take(wide_table, row_ids.astype(jnp.int32), axis=0)
        return jnp.einsum("ckb,kba->ca", taken_rows, weights, precision=lax.Precision.HIGHEST)

    outputs = lax.map(one_block, (block_cols, block_ids))
    return jnp.transpose(outputs, (1, 0, 2)).reshape(row_count, block_total * block_width)


def reference(amplitudes, double_occ, up_cols, up_ids, up_blocks, down_cols, down_ids, down_blocks):
    onsite = coupling * double_occ.astype(jnp.float32) - center

    def apply_scaled(current):
        rounded = lax.optimization_barrier(current.astype(jnp.bfloat16))
        up_hop = hop_last(rounded.T, up_cols, up_ids, up_blocks).T
        down_hop = hop_last(rounded, down_cols, down_ids, down_blocks)
        return (onsite * current + up_hop + down_hop) / half_span

    first = apply_scaled(amplitudes)
    return 2.0 * apply_scaled(first) - amplitudes
```

```python
import jax
import jax.numpy as jnp
from jax import lax
from jax.experimental import pallas as pl
from jax.experimental.pallas import tpu as pltpu
from jax.sharding import PartitionSpec as P

coupling = 0.5
center = 2.0
half_span = 2.0

LANES = 128


def block_order(block_cols, block_ids, shared_count):
    matched = block_ids[:, :, None] == jnp.arange(shared_count, dtype=jnp.int32)[None, None, :]
    return jnp.sum(jnp.where(matched, block_cols[:, :, None], 0), axis=1)


def doubled_table(shared_table):
    shared_count, block_width, _ = shared_table.shape
    wide = jnp.broadcast_to(shared_table[:, None], (shared_count, 2, block_width, block_width))
    return wide.reshape(shared_count * 2 * block_width, block_width)


def _stage_row(idx_ref, base, src_ref, stage_ref, row0, rows, shared_count, half_of_lane):
    for s in range(shared_count):
        c = idx_ref[base + s]
        piece = src_ref[lax.shift_right_logical(c, 1)]
        keep = half_of_lane == (c & 1)
        stage_ref[row0:row0 + rows, s * LANES:(s + 1) * LANES] = jnp.where(
            keep, piece, jnp.zeros_like(piece)
        )


def up_kernel(idx_ref, x_ref, w_ref, o_ref, stage_ref):
    pairs, n, _ = x_ref.shape
    block_width = w_ref.shape[1]
    shared_count = w_ref.shape[0] // LANES
    rows_per_chunk = stage_ref.shape[0] // n
    half_of_lane = jnp.where(
        lax.broadcasted_iota(jnp.int32, (n, LANES), 1) >= block_width, 1, 0
    )

    def chunk(g, carry):
        for rr in range(rows_per_chunk):
            r = g * rows_per_chunk + rr
            _stage_row(idx_ref, r * shared_count, x_ref, stage_ref, rr * n, n,
                       shared_count, half_of_lane)
        res = jnp.dot(stage_ref[...], w_ref[...], preferred_element_type=jnp.float32)
        for rr in range(0, rows_per_chunk, 2):
            i = (g * rows_per_chunk + rr) // 2
            o_ref[i, :, 0:block_width] = res[rr * n:(rr + 1) * n]
            o_ref[i, :, block_width:2 * block_width] = res[(rr + 1) * n:(rr + 2) * n]
        return carry

    lax.fori_loop(0, 2 * pairs // rows_per_chunk, chunk, 0)


def down_kernel(idx_ref, g_ref, w_ref, o_ref, stage_ref):
    _, rows, _ = g_ref.shape
    block_width = w_ref.shape[1]
    shared_count = w_ref.shape[0] // LANES
    own_blocks = o_ref.shape[1] // block_width
    half_of_lane = jnp.where(
        lax.broadcasted_iota(jnp.int32, (rows, LANES), 1) >= block_width, 1, 0
    )
    for r in range(own_blocks):
        _stage_row(idx_ref, r * shared_count, g_ref, stage_ref, 0, rows,
                   shared_count, half_of_lane)
        o_ref[:, r * block_width:(r + 1) * block_width] = jnp.dot(
            stage_ref[...], w_ref[...], preferred_element_type=jnp.float32
        )


def up_hop(idx, x, w):
    pairs, n, _ = x.shape
    rows_per_chunk = 8
    return pl.pallas_call(
        up_kernel,
        out_shape=jax.ShapeDtypeStruct((pairs, n, LANES), jnp.float32),
        in_specs=[
            pl.BlockSpec(memory_space=pltpu.SMEM),
            pl.BlockSpec(memory_space=pltpu.VMEM),
            pl.BlockSpec(memory_space=pltpu.VMEM),
        ],
        out_specs=pl.BlockSpec(memory_space=pltpu.VMEM),
        scratch_shapes=[pltpu.VMEM((rows_per_chunk * n, w.shape[0]), jnp.bfloat16)],
    )(idx, x, w)


def down_hop(idx, g, w, own_cols):
    _, rows, _ = g.shape
    return pl.pallas_call(
        down_kernel,
        out_shape=jax.ShapeDtypeStruct((rows, own_cols), jnp.float32),
        in_specs=[
            pl.BlockSpec(memory_space=pltpu.SMEM),
            pl.BlockSpec(memory_space=pltpu.VMEM),
            pl.BlockSpec(memory_space=pltpu.VMEM),
        ],
        out_specs=pl.BlockSpec(memory_space=pltpu.VMEM),
        scratch_shapes=[pltpu.VMEM((rows, w.shape[0]), jnp.bfloat16)],
    )(idx, g, w)


def body(amplitudes, double_occ, up_cols, up_ids, up_blocks, down_cols, down_ids, down_blocks):
    shared_count = up_blocks.shape[0]
    block_width = up_blocks.shape[1]
    local_rows, local_cols = amplitudes.shape
    up_count = lax.axis_size("up")
    own_blocks = local_cols // block_width
    up_idx = block_order(up_cols, up_ids, shared_count).reshape(-1)
    down_order = block_order(down_cols, down_ids, shared_count)
    down_idx = lax.dynamic_slice_in_dim(
        down_order, lax.axis_index("down") * own_blocks, own_blocks, 0
    ).reshape(-1)
    up_table = doubled_table(up_blocks)
    down_table = doubled_table(down_blocks)
    onsite = coupling * double_occ.astype(jnp.float32) - center

    def up_part(rounded):
        sectioned = rounded.T.reshape(up_count, local_cols // up_count, local_rows)
        received = lax.all_to_all(sectioned, "up", 0, 0, tiled=True)
        hopped = up_hop(up_idx, received, up_table)
        returned = lax.all_to_all(hopped, "up", 0, 0, tiled=True)
        return returned.reshape(local_cols, local_rows).T

    def down_part(rounded):
        paired = rounded.reshape(local_rows, local_cols // LANES, LANES).transpose(1, 0, 2)
        gathered = lax.all_gather(paired, "down", axis=0, tiled=True)
        return down_hop(down_idx, gathered, down_table, local_cols)

    def apply_scaled(current):
        rounded = current.astype(jnp.bfloat16)
        return (onsite * current + up_part(rounded) + down_part(rounded)) / half_span

    first = apply_scaled(amplitudes)
    return 2.0 * apply_scaled(first) - amplitudes


def solution(mesh):
    placed = (P("up", "down"), P("up", "down"), P(), P(), P(), P(), P(), P())
    return jax.shard_map(
        body, mesh=mesh, in_specs=placed, out_specs=P("up", "down"), check_vma=False
    )
```

```python
import jax
import jax.numpy as jnp
from jax import lax
from jax.experimental import pallas as pl
from jax.experimental.pallas import tpu as pltpu
from jax.sharding import PartitionSpec as P

coupling = 0.5
center = 2.0
half_span = 2.0

LANES = 128


def block_order(block_cols, block_ids, shared_count):
    matched = block_ids[:, :, None] == jnp.arange(shared_count, dtype=jnp.int32)[None, None, :]
    return jnp.sum(jnp.where(matched, block_cols[:, :, None], 0), axis=1)


def doubled_table(shared_table):
    shared_count, block_width, _ = shared_table.shape
    wide = jnp.broadcast_to(shared_table[:, None], (shared_count, 2, block_width, block_width))
    return wide.reshape(shared_count * 2 * block_width, block_width)


def _stage_row(idx_ref, base, src_ref, stage_ref, row0, rows, shared_count, half_of_lane):
    for s in range(shared_count):
        c = idx_ref[base + s]
        piece = src_ref[lax.shift_right_logical(c, 1)]
        keep = half_of_lane == (c & 1)
        stage_ref[row0:row0 + rows, s * LANES:(s + 1) * LANES] = jnp.where(
            keep, piece, jnp.zeros_like(piece)
        )


def up_kernel(idx_ref, x_ref, w_ref, o_ref, stage_ref):
    pairs, n, _ = x_ref.shape
    block_width = w_ref.shape[1]
    shared_count = w_ref.shape[0] // LANES
    rows_per_chunk = stage_ref.shape[0] // n
    half_of_lane = jnp.where(
        lax.broadcasted_iota(jnp.int32, (n, LANES), 1) >= block_width, 1, 0
    )

    def chunk(g, carry):
        for rr in range(rows_per_chunk):
            r = g * rows_per_chunk + rr
            _stage_row(idx_ref, r * shared_count, x_ref, stage_ref, rr * n, n,
                       shared_count, half_of_lane)
        res = jnp.dot(stage_ref[...], w_ref[...], preferred_element_type=jnp.float32)
        for rr in range(0, rows_per_chunk, 2):
            i = (g * rows_per_chunk + rr) // 2
            o_ref[i, :, 0:block_width] = res[rr * n:(rr + 1) * n]
            o_ref[i, :, block_width:2 * block_width] = res[(rr + 1) * n:(rr + 2) * n]
        return carry

    lax.fori_loop(0, 2 * pairs // rows_per_chunk, chunk, 0)


def down_kernel(idx_ref, g_ref, w_ref, o_ref, stage_ref):
    _, rows, _ = g_ref.shape
    block_width = w_ref.shape[1]
    shared_count = w_ref.shape[0] // LANES
    own_blocks = o_ref.shape[1] // block_width
    half_of_lane = jnp.where(
        lax.broadcasted_iota(jnp.int32, (rows, LANES), 1) >= block_width, 1, 0
    )
    for r in range(own_blocks):
        _stage_row(idx_ref, r * shared_count, g_ref, stage_ref, 0, rows,
                   shared_count, half_of_lane)
        o_ref[:, r * block_width:(r + 1) * block_width] = jnp.dot(
            stage_ref[...], w_ref[...], preferred_element_type=jnp.float32
        )


def up_hop(idx, x, w):
    pairs, n, _ = x.shape
    rows_per_chunk = 8
    return pl.pallas_call(
        up_kernel,
        out_shape=jax.ShapeDtypeStruct((pairs, n, LANES), jnp.float32),
        in_specs=[
            pl.BlockSpec(memory_space=pltpu.SMEM),
            pl.BlockSpec(memory_space=pltpu.VMEM),
            pl.BlockSpec(memory_space=pltpu.VMEM),
        ],
        out_specs=pl.BlockSpec(memory_space=pltpu.VMEM),
        scratch_shapes=[pltpu.VMEM((rows_per_chunk * n, w.shape[0]), jnp.bfloat16)],
    )(idx, x, w)


def down_hop(idx, g, w, own_cols):
    _, rows, _ = g.shape
    return pl.pallas_call(
        down_kernel,
        out_shape=jax.ShapeDtypeStruct((rows, own_cols), jnp.float32),
        in_specs=[
            pl.BlockSpec(memory_space=pltpu.SMEM),
            pl.BlockSpec(memory_space=pltpu.VMEM),
            pl.BlockSpec(memory_space=pltpu.VMEM),
        ],
        out_specs=pl.BlockSpec(memory_space=pltpu.VMEM),
        scratch_shapes=[pltpu.VMEM((rows, w.shape[0]), jnp.bfloat16)],
    )(idx, g, w)


def body(amplitudes, double_occ, up_cols, up_ids, up_blocks, down_cols, down_ids, down_blocks):
    shared_count = up_blocks.shape[0]
    block_width = up_blocks.shape[1]
    local_rows, local_cols = amplitudes.shape
    up_count = lax.axis_size("up")
    own_blocks = local_cols // block_width
    up_idx = block_order(up_cols, up_ids, shared_count).reshape(-1)
    down_order = block_order(down_cols, down_ids, shared_count)
    down_idx = lax.dynamic_slice_in_dim(
        down_order, lax.axis_index("down") * own_blocks, own_blocks, 0
    ).reshape(-1)
    up_table = doubled_table(up_blocks)
    down_table = doubled_table(down_blocks)
    onsite = coupling * double_occ.astype(jnp.float32) - center
    down_count = lax.axis_size("down")
    col_chunk = local_cols // up_count

    def to_columns(values):
        return values.T.reshape(up_count, col_chunk, local_rows)

    def to_rows(pieces):
        return pieces.reshape(local_cols, local_rows).T

    def exchange_up(pieces):
        return lax.all_to_all(pieces, "up", 0, 0, tiled=True)

    def down_part(rounded):
        paired = rounded.reshape(local_rows, local_cols // LANES, LANES).transpose(1, 0, 2)
        copies = jnp.broadcast_to(paired[None], (down_count,) + paired.shape)
        gathered = lax.all_to_all(copies, "down", 0, 0, tiled=True)
        gathered = gathered.reshape((-1,) + paired.shape[1:])
        return down_hop(down_idx, gathered, down_table, local_cols)

    rounded0 = amplitudes.astype(jnp.bfloat16)
    up0_cols = up_hop(up_idx, exchange_up(to_columns(rounded0)), up_table)
    partial_rows = onsite * amplitudes + down_part(rounded0)
    both = exchange_up(jnp.concatenate([to_columns(partial_rows), up0_cols], axis=1))
    partial_cols = both[:, :col_chunk]
    up0_rows = to_rows(both[:, col_chunk:])
    first_cols = (partial_cols + up0_cols) / half_span
    first_rows = (partial_rows + up0_rows) / half_span

    up1_cols = up_hop(up_idx, first_cols.astype(jnp.bfloat16), up_table)
    down1_rows = down_part(first_rows.astype(jnp.bfloat16))
    up1_rows = to_rows(exchange_up(up1_cols))
    return 2.0 * ((onsite * first_rows + up1_rows + down1_rows) / half_span) - amplitudes


def solution(mesh):
    placed = (P("up", "down"), P("up", "down"), P(), P(), P(), P(), P(), P())
    return jax.shard_map(
        body, mesh=mesh, in_specs=placed, out_specs=P("up", "down"), check_vma=False
    )
```

```python
import jax
import jax.numpy as jnp
from jax import lax
from jax.experimental import pallas as pl
from jax.experimental.pallas import tpu as pltpu
from jax.sharding import PartitionSpec as P

coupling = 0.5
center = 2.0
half_span = 2.0

LANES = 128


def block_order(block_cols, block_ids, shared_count):
    matched = block_ids[:, :, None] == jnp.arange(shared_count, dtype=jnp.int32)[None, None, :]
    return jnp.sum(jnp.where(matched, block_cols[:, :, None], 0), axis=1)


def doubled_table(shared_table):
    shared_count, block_width, _ = shared_table.shape
    wide = jnp.broadcast_to(shared_table[:, None], (shared_count, 2, block_width, block_width))
    return wide.reshape(shared_count * 2 * block_width, block_width)


def _stage_row(idx_ref, base, src_ref, stage_ref, row0, rows, shared_count, half_of_lane):
    for s in range(shared_count):
        c = idx_ref[base + s]
        piece = src_ref[lax.shift_right_logical(c, 1)]
        keep = half_of_lane == (c & 1)
        stage_ref[row0:row0 + rows, s * LANES:(s + 1) * LANES] = jnp.where(
            keep, piece, jnp.zeros_like(piece)
        )


def up_kernel(idx_ref, x_ref, w_ref, o_ref, stage_ref):
    pairs, n, _ = x_ref.shape
    block_width = w_ref.shape[1]
    shared_count = w_ref.shape[0] // LANES
    rows_per_chunk = stage_ref.shape[0] // n
    half_of_lane = jnp.where(
        lax.broadcasted_iota(jnp.int32, (n, LANES), 1) >= block_width, 1, 0
    )

    def chunk(g, carry):
        for rr in range(rows_per_chunk):
            r = g * rows_per_chunk + rr
            _stage_row(idx_ref, r * shared_count, x_ref, stage_ref, rr * n, n,
                       shared_count, half_of_lane)
        res = jnp.dot(stage_ref[...], w_ref[...], preferred_element_type=jnp.float32)
        for rr in range(0, rows_per_chunk, 2):
            i = (g * rows_per_chunk + rr) // 2
            o_ref[i, :, 0:block_width] = res[rr * n:(rr + 1) * n]
            o_ref[i, :, block_width:2 * block_width] = res[(rr + 1) * n:(rr + 2) * n]
        return carry

    lax.fori_loop(0, 2 * pairs // rows_per_chunk, chunk, 0)


def down_kernel(idx_ref, g_ref, w_ref, o_ref, stage_ref):
    _, rows, _ = g_ref.shape
    block_width = w_ref.shape[1]
    shared_count = w_ref.shape[0] // LANES
    own_blocks = o_ref.shape[1] // block_width
    half_of_lane = jnp.where(
        lax.broadcasted_iota(jnp.int32, (rows, LANES), 1) >= block_width, 1, 0
    )
    for r in range(own_blocks):
        _stage_row(idx_ref, r * shared_count, g_ref, stage_ref, 0, rows,
                   shared_count, half_of_lane)
        o_ref[:, r * block_width:(r + 1) * block_width] = jnp.dot(
            stage_ref[...], w_ref[...], preferred_element_type=jnp.float32
        )


def up_hop(idx, x, w):
    pairs, n, _ = x.shape
    rows_per_chunk = 8
    return pl.pallas_call(
        up_kernel,
        out_shape=jax.ShapeDtypeStruct((pairs, n, LANES), jnp.float32),
        in_specs=[
            pl.BlockSpec(memory_space=pltpu.SMEM),
            pl.BlockSpec(memory_space=pltpu.VMEM),
            pl.BlockSpec(memory_space=pltpu.VMEM),
        ],
        out_specs=pl.BlockSpec(memory_space=pltpu.VMEM),
        scratch_shapes=[pltpu.VMEM((rows_per_chunk * n, w.shape[0]), jnp.bfloat16)],
    )(idx, x, w)


def down_hop(idx, g, w, own_cols):
    _, rows, _ = g.shape
    return pl.pallas_call(
        down_kernel,
        out_shape=jax.ShapeDtypeStruct((rows, own_cols), jnp.float32),
        in_specs=[
            pl.BlockSpec(memory_space=pltpu.SMEM),
            pl.BlockSpec(memory_space=pltpu.VMEM),
            pl.BlockSpec(memory_space=pltpu.VMEM),
        ],
        out_specs=pl.BlockSpec(memory_space=pltpu.VMEM),
        scratch_shapes=[pltpu.VMEM((rows, w.shape[0]), jnp.bfloat16)],
    )(idx, g, w)


def body(amplitudes, double_occ, up_cols, up_ids, up_blocks, down_cols, down_ids, down_blocks):
    shared_count = up_blocks.shape[0]
    block_width = up_blocks.shape[1]
    local_rows, local_cols = amplitudes.shape
    up_count = lax.axis_size("up")
    own_blocks = local_cols // block_width
    up_idx = block_order(up_cols, up_ids, shared_count).reshape(-1)
    down_order = block_order(down_cols, down_ids, shared_count)
    down_idx = lax.dynamic_slice_in_dim(
        down_order, lax.axis_index("down") * own_blocks, own_blocks, 0
    ).reshape(-1)
    up_table = doubled_table(up_blocks)
    down_table = doubled_table(down_blocks)
    onsite = coupling * double_occ.astype(jnp.float32) - center
    col_chunk = local_cols // up_count

    def to_columns(values):
        return values.T.reshape(up_count, col_chunk, local_rows)

    def to_rows(pieces):
        return pieces.reshape(local_cols, local_rows).T

    def exchange_up(pieces):
        return lax.all_to_all(pieces, "up", 0, 0, tiled=True)

    def down_part(rounded):
        paired = rounded.reshape(local_rows, local_cols // LANES, LANES).transpose(1, 0, 2)
        gathered = lax.all_gather(paired, "down", axis=0, tiled=True)
        return down_hop(down_idx, gathered, down_table, local_cols)

    rounded0 = amplitudes.astype(jnp.bfloat16)
    up0_cols = up_hop(up_idx, exchange_up(to_columns(rounded0)), up_table)
    partial_rows = onsite * amplitudes + down_part(rounded0)
    both = exchange_up(jnp.concatenate([to_columns(partial_rows), up0_cols], axis=1))
    partial_cols = both[:, :col_chunk]
    up0_rows = to_rows(both[:, col_chunk:])
    first_cols = (partial_cols + up0_cols) / half_span
    first_rows = (partial_rows + up0_rows) / half_span

    up1_cols = up_hop(up_idx, first_cols.astype(jnp.bfloat16), up_table)
    down1_rows = down_part(first_rows.astype(jnp.bfloat16))
    up1_rows = to_rows(exchange_up(up1_cols))
    return 2.0 * ((onsite * first_rows + up1_rows + down1_rows) / half_span) - amplitudes


def solution(mesh):
    placed = (P("up", "down"), P("up", "down"), P(), P(), P(), P(), P(), P())
    return jax.shard_map(
        body, mesh=mesh, in_specs=placed, out_specs=P("up", "down"), check_vma=False
    )
```

```python
import jax
import jax.numpy as jnp
from jax import lax
from jax.experimental import pallas as pl
from jax.experimental.pallas import tpu as pltpu
from jax.sharding import PartitionSpec as P

coupling = 0.5
center = 2.0
half_span = 2.0

LANES = 128


def block_order(block_cols, block_ids, shared_count):
    matched = block_ids[:, :, None] == jnp.arange(shared_count, dtype=jnp.int32)[None, None, :]
    return jnp.sum(jnp.where(matched, block_cols[:, :, None], 0), axis=1)


def doubled_table(shared_table):
    shared_count, block_width, _ = shared_table.shape
    wide = jnp.broadcast_to(shared_table[:, None], (shared_count, 2, block_width, block_width))
    return wide.reshape(shared_count * 2 * block_width, block_width)


def _stage_row(idx_ref, base, src_ref, stage_ref, row0, rows, shared_count, half_of_lane):
    for s in range(shared_count):
        c = idx_ref[base + s]
        piece = src_ref[lax.shift_right_logical(c, 1)]
        keep = half_of_lane == (c & 1)
        stage_ref[row0:row0 + rows, s * LANES:(s + 1) * LANES] = jnp.where(
            keep, piece, jnp.zeros_like(piece)
        )


def up_kernel(idx_ref, x_ref, w_ref, o_ref, stage_ref):
    pairs, n, _ = x_ref.shape
    block_width = w_ref.shape[1]
    shared_count = w_ref.shape[0] // LANES
    rows_per_chunk = stage_ref.shape[0] // n
    half_of_lane = jnp.where(
        lax.broadcasted_iota(jnp.int32, (n, LANES), 1) >= block_width, 1, 0
    )

    def chunk(g, carry):
        for rr in range(rows_per_chunk):
            r = g * rows_per_chunk + rr
            _stage_row(idx_ref, r * shared_count, x_ref, stage_ref, rr * n, n,
                       shared_count, half_of_lane)
        res = jnp.dot(stage_ref[...], w_ref[...], preferred_element_type=jnp.float32)
        for rr in range(0, rows_per_chunk, 2):
            i = (g * rows_per_chunk + rr) // 2
            o_ref[i, :, 0:block_width] = res[rr * n:(rr + 1) * n]
            o_ref[i, :, block_width:2 * block_width] = res[(rr + 1) * n:(rr + 2) * n]
        return carry

    lax.fori_loop(0, 2 * pairs // rows_per_chunk, chunk, 0)


def down_kernel(idx_ref, g_ref, w_ref, o_ref, stage_ref):
    _, rows, _ = g_ref.shape
    block_width = w_ref.shape[1]
    shared_count = w_ref.shape[0] // LANES
    own_blocks = o_ref.shape[1] // block_width
    half_of_lane = jnp.where(
        lax.broadcasted_iota(jnp.int32, (rows, LANES), 1) >= block_width, 1, 0
    )
    for r in range(own_blocks):
        _stage_row(idx_ref, r * shared_count, g_ref, stage_ref, 0, rows,
                   shared_count, half_of_lane)
        o_ref[:, r * block_width:(r + 1) * block_width] = jnp.dot(
            stage_ref[...], w_ref[...], preferred_element_type=jnp.float32
        )


def up_hop(idx, x, w):
    pairs, n, _ = x.shape
    rows_per_chunk = 8
    return pl.pallas_call(
        up_kernel,
        out_shape=jax.ShapeDtypeStruct((pairs, n, LANES), jnp.float32),
        in_specs=[
            pl.BlockSpec(memory_space=pltpu.SMEM),
            pl.BlockSpec(memory_space=pltpu.VMEM),
            pl.BlockSpec(memory_space=pltpu.VMEM),
        ],
        out_specs=pl.BlockSpec(memory_space=pltpu.VMEM),
        scratch_shapes=[pltpu.VMEM((rows_per_chunk * n, w.shape[0]), jnp.bfloat16)],
    )(idx, x, w)


def down_hop(idx, g, w, own_cols):
    _, rows, _ = g.shape
    return pl.pallas_call(
        down_kernel,
        out_shape=jax.ShapeDtypeStruct((rows, own_cols), jnp.float32),
        in_specs=[
            pl.BlockSpec(memory_space=pltpu.SMEM),
            pl.BlockSpec(memory_space=pltpu.VMEM),
            pl.BlockSpec(memory_space=pltpu.VMEM),
        ],
        out_specs=pl.BlockSpec(memory_space=pltpu.VMEM),
        scratch_shapes=[pltpu.VMEM((rows, w.shape[0]), jnp.bfloat16)],
    )(idx, g, w)


def body(amplitudes, double_occ, up_cols, up_ids, up_blocks, down_cols, down_ids, down_blocks):
    shared_count = up_blocks.shape[0]
    block_width = up_blocks.shape[1]
    local_rows, local_cols = amplitudes.shape
    up_count = lax.axis_size("up")
    own_blocks = local_cols // block_width
    up_idx = block_order(up_cols, up_ids, shared_count).reshape(-1)
    down_order = block_order(down_cols, down_ids, shared_count)
    down_idx = lax.dynamic_slice_in_dim(
        down_order, lax.axis_index("down") * own_blocks, own_blocks, 0
    ).reshape(-1)
    down_count = lax.axis_size("down")
    pairs_per_device = local_cols // LANES
    split = pairs_per_device // 2
    pair = down_idx >> 1
    source, slot = pair // pairs_per_device, pair % pairs_per_device
    in_second = slot >= split
    new_pair = jnp.where(
        in_second,
        down_count * split + source * (pairs_per_device - split) + slot - split,
        source * split + slot,
    )
    down_idx = new_pair * 2 + (down_idx & 1)
    up_table = doubled_table(up_blocks)
    down_table = doubled_table(down_blocks)
    onsite = coupling * double_occ.astype(jnp.float32) - center
    col_chunk = local_cols // up_count

    def to_columns(values):
        return values.T.reshape(up_count, col_chunk, local_rows)

    def to_rows(pieces):
        return pieces.reshape(local_cols, local_rows).T

    def exchange_up(pieces):
        return lax.all_to_all(pieces, "up", 0, 0, tiled=True)

    def down_part(rounded):
        paired = rounded.reshape(local_rows, local_cols // LANES, LANES).transpose(1, 0, 2)
        halves = [
            lax.all_gather(paired[:split], "down", axis=0, tiled=True),
            lax.all_gather(paired[split:], "down", axis=0, tiled=True),
        ]
        return down_hop(down_idx, jnp.concatenate(halves, axis=0), down_table, local_cols)

    rounded0 = amplitudes.astype(jnp.bfloat16)
    up0_cols = up_hop(up_idx, exchange_up(to_columns(rounded0)), up_table)
    partial_rows = onsite * amplitudes + down_part(rounded0)
    both = exchange_up(jnp.concatenate([to_columns(partial_rows), up0_cols], axis=1))
    partial_cols = both[:, :col_chunk]
    up0_rows = to_rows(both[:, col_chunk:])
    first_cols = (partial_cols + up0_cols) / half_span
    first_rows = (partial_rows + up0_rows) / half_span

    up1_cols = up_hop(up_idx, first_cols.astype(jnp.bfloat16), up_table)
    down1_rows = down_part(first_rows.astype(jnp.bfloat16))
    up1_rows = to_rows(exchange_up(up1_cols))
    return 2.0 * ((onsite * first_rows + up1_rows + down1_rows) / half_span) - amplitudes


def solution(mesh):
    placed = (P("up", "down"), P("up", "down"), P(), P(), P(), P(), P(), P())
    return jax.shard_map(
        body, mesh=mesh, in_specs=placed, out_specs=P("up", "down"), check_vma=False
    )
```

```python
import jax
import jax.numpy as jnp
from jax import lax
from jax.experimental import pallas as pl
from jax.experimental.pallas import tpu as pltpu
from jax.sharding import PartitionSpec as P

coupling = 0.5
center = 2.0
half_span = 2.0

LANES = 128


def block_order(block_cols, block_ids, shared_count):
    matched = block_ids[:, :, None] == jnp.arange(shared_count, dtype=jnp.int32)[None, None, :]
    return jnp.sum(jnp.where(matched, block_cols[:, :, None], 0), axis=1)


def _fill_rolled(src_ref, src2_ref):
    half = src_ref.shape[-1] // 2

    def one(i, carry):
        piece = src_ref[i]
        src2_ref[0, i] = piece
        src2_ref[1, i] = pltpu.roll(piece, half, 1)
        return carry

    lax.fori_loop(0, src_ref.shape[0], one, 0)


def _stage_row(idx_ref, base, src2_ref, stage_ref, row0, rows, shared_count, low_lanes):
    for t in range(shared_count // 2):
        ce = idx_ref[base + 2 * t]
        co = idx_ref[base + 2 * t + 1]
        even = src2_ref[ce & 1, lax.shift_right_logical(ce, 1)]
        odd = src2_ref[(co & 1) ^ 1, lax.shift_right_logical(co, 1)]
        stage_ref[row0:row0 + rows, t * LANES:(t + 1) * LANES] = jnp.where(low_lanes, even, odd)


def up_kernel(idx_ref, x_ref, w_ref, o_ref, src2_ref, stage_ref):
    pairs, n, _ = x_ref.shape
    block_width = w_ref.shape[1]
    shared_count = w_ref.shape[0] // block_width
    rows_per_chunk = stage_ref.shape[0] // n
    low_lanes = lax.broadcasted_iota(jnp.int32, (n, LANES), 1) < block_width
    _fill_rolled(x_ref, src2_ref)

    def chunk(g, carry):
        for rr in range(rows_per_chunk):
            r = g * rows_per_chunk + rr
            _stage_row(idx_ref, r * shared_count, src2_ref, stage_ref, rr * n, n,
                       shared_count, low_lanes)
        res = jnp.dot(stage_ref[...], w_ref[...], preferred_element_type=jnp.float32)
        for rr in range(0, rows_per_chunk, 2):
            i = (g * rows_per_chunk + rr) // 2
            o_ref[i, :, 0:block_width] = res[rr * n:(rr + 1) * n]
            o_ref[i, :, block_width:2 * block_width] = res[(rr + 1) * n:(rr + 2) * n]
        return carry

    lax.fori_loop(0, 2 * pairs // rows_per_chunk, chunk, 0)


def down_kernel(idx_ref, g_ref, w_ref, o_ref, src2_ref, stage_ref):
    _, rows, _ = g_ref.shape
    block_width = w_ref.shape[1]
    shared_count = w_ref.shape[0] // block_width
    own_blocks = o_ref.shape[1] // block_width
    low_lanes = lax.broadcasted_iota(jnp.int32, (rows, LANES), 1) < block_width
    _fill_rolled(g_ref, src2_ref)
    for r in range(own_blocks):
        _stage_row(idx_ref, r * shared_count, src2_ref, stage_ref, 0, rows,
                   shared_count, low_lanes)
        o_ref[:, r * block_width:(r + 1) * block_width] = jnp.dot(
            stage_ref[...], w_ref[...], preferred_element_type=jnp.float32
        )


def up_hop(idx, x, w):
    pairs, n, _ = x.shape
    rows_per_chunk = 8
    return pl.pallas_call(
        up_kernel,
        out_shape=jax.ShapeDtypeStruct((pairs, n, LANES), jnp.float32),
        in_specs=[
            pl.BlockSpec(memory_space=pltpu.SMEM),
            pl.BlockSpec(memory_space=pltpu.VMEM),
            pl.BlockSpec(memory_space=pltpu.VMEM),
        ],
        out_specs=pl.BlockSpec(memory_space=pltpu.VMEM),
        scratch_shapes=[
            pltpu.VMEM((2,) + x.shape, jnp.bfloat16),
            pltpu.VMEM((rows_per_chunk * n, w.shape[0]), jnp.bfloat16),
        ],
    )(idx, x, w)


def down_hop(idx, g, w, own_cols):
    _, rows, _ = g.shape
    return pl.pallas_call(
        down_kernel,
        out_shape=jax.ShapeDtypeStruct((rows, own_cols), jnp.float32),
        in_specs=[
            pl.BlockSpec(memory_space=pltpu.SMEM),
            pl.BlockSpec(memory_space=pltpu.VMEM),
            pl.BlockSpec(memory_space=pltpu.VMEM),
        ],
        out_specs=pl.BlockSpec(memory_space=pltpu.VMEM),
        scratch_shapes=[
            pltpu.VMEM((2,) + g.shape, jnp.bfloat16),
            pltpu.VMEM((rows, w.shape[0]), jnp.bfloat16),
        ],
    )(idx, g, w)


def body(amplitudes, double_occ, up_cols, up_ids, up_blocks, down_cols, down_ids, down_blocks):
    shared_count = up_blocks.shape[0]
    block_width = up_blocks.shape[1]
    local_rows, local_cols = amplitudes.shape
    up_count = lax.axis_size("up")
    own_blocks = local_cols // block_width
    up_idx = block_order(up_cols, up_ids, shared_count).reshape(-1)
    down_order = block_order(down_cols, down_ids, shared_count)
    down_idx = lax.dynamic_slice_in_dim(
        down_order, lax.axis_index("down") * own_blocks, own_blocks, 0
    ).reshape(-1)
    up_table = up_blocks.reshape(shared_count * block_width, block_width)
    down_table = down_blocks.reshape(shared_count * block_width, block_width)
    onsite = coupling * double_occ.astype(jnp.float32) - center
    col_chunk = local_cols // up_count

    def to_columns(values):
        return values.T.reshape(up_count, col_chunk, local_rows)

    def to_rows(pieces):
        return pieces.reshape(local_cols, local_rows).T

    def exchange_up(pieces):
        return lax.all_to_all(pieces, "up", 0, 0, tiled=True)

    def down_part(rounded):
        paired = rounded.reshape(local_rows, local_cols // LANES, LANES).transpose(1, 0, 2)
        gathered = lax.all_gather(paired, "down", axis=0, tiled=True)
        return down_hop(down_idx, gathered, down_table, local_cols)

    rounded0 = amplitudes.astype(jnp.bfloat16)
    up0_cols = up_hop(up_idx, exchange_up(to_columns(rounded0)), up_table)
    partial_rows = onsite * amplitudes + down_part(rounded0)
    both = exchange_up(jnp.concatenate([to_columns(partial_rows), up0_cols], axis=1))
    partial_cols = both[:, :col_chunk]
    up0_rows = to_rows(both[:, col_chunk:])
    first_cols = (partial_cols + up0_cols) / half_span
    first_rows = (partial_rows + up0_rows) / half_span

    up1_cols = up_hop(up_idx, first_cols.astype(jnp.bfloat16), up_table)
    down1_rows = down_part(first_rows.astype(jnp.bfloat16))
    up1_rows = to_rows(exchange_up(up1_cols))
    return 2.0 * ((onsite * first_rows + up1_rows + down1_rows) / half_span) - amplitudes


def solution(mesh):
    placed = (P("up", "down"), P("up", "down"), P(), P(), P(), P(), P(), P())
    return jax.shard_map(
        body, mesh=mesh, in_specs=placed, out_specs=P("up", "down"), check_vma=False
    )
```

```python
import jax
import jax.numpy as jnp
from jax import lax
from jax.experimental import pallas as pl
from jax.experimental.pallas import tpu as pltpu
from jax.sharding import PartitionSpec as P

coupling = 0.5
center = 2.0
half_span = 2.0

LANES = 128


def block_order(block_cols, block_ids, shared_count):
    matched = block_ids[:, :, None] == jnp.arange(shared_count, dtype=jnp.int32)[None, None, :]
    return jnp.sum(jnp.where(matched, block_cols[:, :, None], 0), axis=1)


def _fill_rolled(src_ref, src2_ref):
    pairs = src_ref.shape[0]
    half = src_ref.shape[-1] // 2

    def one(i, carry):
        piece = src_ref[i]
        src2_ref[i] = piece
        src2_ref[pairs + i] = pltpu.roll(piece, half, 1)
        return carry

    lax.fori_loop(0, pairs, one, 0)


def _stage_row(idx_ref, base, src2_ref, stage_ref, row0, rows, shared_count, half):
    for t in range(shared_count // 2):
        even = idx_ref[base + 2 * t]
        odd = idx_ref[base + 2 * t + 1]
        stage_ref[row0:row0 + rows, t * LANES:t * LANES + half] = src2_ref[even, :, 0:half]
        stage_ref[row0:row0 + rows, t * LANES + half:(t + 1) * LANES] = src2_ref[odd, :, half:LANES]


def source_index(order, pairs):
    parity = jnp.arange(order.shape[-1], dtype=jnp.int32) % 2
    return ((order & 1) ^ parity) * pairs + (order >> 1)


def up_kernel(idx_ref, x_ref, w_ref, o_ref, src2_ref, stage_ref):
    pairs, n, _ = x_ref.shape
    block_width = w_ref.shape[1]
    shared_count = w_ref.shape[0] // block_width
    rows_per_chunk = stage_ref.shape[0] // n
    _fill_rolled(x_ref, src2_ref)

    def chunk(g, carry):
        for rr in range(rows_per_chunk):
            r = g * rows_per_chunk + rr
            _stage_row(idx_ref, r * shared_count, src2_ref, stage_ref, rr * n, n,
                       shared_count, block_width)
        res = jnp.dot(stage_ref[...], w_ref[...], preferred_element_type=jnp.float32)
        for rr in range(0, rows_per_chunk, 2):
            i = (g * rows_per_chunk + rr) // 2
            o_ref[i, :, 0:block_width] = res[rr * n:(rr + 1) * n]
            o_ref[i, :, block_width:2 * block_width] = res[(rr + 1) * n:(rr + 2) * n]
        return carry

    lax.fori_loop(0, 2 * pairs // rows_per_chunk, chunk, 0)


def down_kernel(idx_ref, g_ref, w_ref, o_ref, src2_ref, stage_ref):
    _, rows, _ = g_ref.shape
    block_width = w_ref.shape[1]
    shared_count = w_ref.shape[0] // block_width
    own_blocks = o_ref.shape[1] // block_width
    _fill_rolled(g_ref, src2_ref)
    for r in range(own_blocks):
        _stage_row(idx_ref, r * shared_count, src2_ref, stage_ref, 0, rows,
                   shared_count, block_width)
        o_ref[:, r * block_width:(r + 1) * block_width] = jnp.dot(
            stage_ref[...], w_ref[...], preferred_element_type=jnp.float32
        )


def up_hop(idx, x, w):
    pairs, n, _ = x.shape
    rows_per_chunk = 8
    return pl.pallas_call(
        up_kernel,
        out_shape=jax.ShapeDtypeStruct((pairs, n, LANES), jnp.float32),
        in_specs=[
            pl.BlockSpec(memory_space=pltpu.SMEM),
            pl.BlockSpec(memory_space=pltpu.VMEM),
            pl.BlockSpec(memory_space=pltpu.VMEM),
        ],
        out_specs=pl.BlockSpec(memory_space=pltpu.VMEM),
        scratch_shapes=[
            pltpu.VMEM((2 * pairs, n, LANES), jnp.bfloat16),
            pltpu.VMEM((rows_per_chunk * n, w.shape[0]), jnp.bfloat16),
        ],
    )(idx, x, w)


def down_hop(idx, g, w, own_cols):
    _, rows, _ = g.shape
    return pl.pallas_call(
        down_kernel,
        out_shape=jax.ShapeDtypeStruct((rows, own_cols), jnp.float32),
        in_specs=[
            pl.BlockSpec(memory_space=pltpu.SMEM),
            pl.BlockSpec(memory_space=pltpu.VMEM),
            pl.BlockSpec(memory_space=pltpu.VMEM),
        ],
        out_specs=pl.BlockSpec(memory_space=pltpu.VMEM),
        scratch_shapes=[
            pltpu.VMEM((2 * g.shape[0], rows, LANES), jnp.bfloat16),
            pltpu.VMEM((rows, w.shape[0]), jnp.bfloat16),
        ],
    )(idx, g, w)


def body(amplitudes, double_occ, up_cols, up_ids, up_blocks, down_cols, down_ids, down_blocks):
    shared_count = up_blocks.shape[0]
    block_width = up_blocks.shape[1]
    local_rows, local_cols = amplitudes.shape
    up_count = lax.axis_size("up")
    own_blocks = local_cols // block_width
    up_idx = source_index(block_order(up_cols, up_ids, shared_count), up_count).reshape(-1)
    down_order = block_order(down_cols, down_ids, shared_count)
    down_idx = source_index(lax.dynamic_slice_in_dim(
        down_order, lax.axis_index("down") * own_blocks, own_blocks, 0
    ), lax.axis_size("down") * local_cols // LANES).reshape(-1)
    up_table = up_blocks.reshape(shared_count * block_width, block_width)
    down_table = down_blocks.reshape(shared_count * block_width, block_width)
    onsite = coupling * double_occ.astype(jnp.float32) - center
    col_chunk = local_cols // up_count

    def to_columns(values):
        return values.T.reshape(up_count, col_chunk, local_rows)

    def to_rows(pieces):
        return pieces.reshape(local_cols, local_rows).T

    def exchange_up(pieces):
        return lax.all_to_all(pieces, "up", 0, 0, tiled=True)

    def down_part(rounded):
        paired = rounded.reshape(local_rows, local_cols // LANES, LANES).transpose(1, 0, 2)
        gathered = lax.all_gather(paired, "down", axis=0, tiled=True)
        return down_hop(down_idx, gathered, down_table, local_cols)

    rounded0 = amplitudes.astype(jnp.bfloat16)
    up0_cols = up_hop(up_idx, exchange_up(to_columns(rounded0)), up_table)
    partial_rows = onsite * amplitudes + down_part(rounded0)
    both = exchange_up(jnp.concatenate([to_columns(partial_rows), up0_cols], axis=1))
    partial_cols = both[:, :col_chunk]
    up0_rows = to_rows(both[:, col_chunk:])
    first_cols = (partial_cols + up0_cols) / half_span
    first_rows = (partial_rows + up0_rows) / half_span

    up1_cols = up_hop(up_idx, first_cols.astype(jnp.bfloat16), up_table)
    down1_rows = down_part(first_rows.astype(jnp.bfloat16))
    up1_rows = to_rows(exchange_up(up1_cols))
    return 2.0 * ((onsite * first_rows + up1_rows + down1_rows) / half_span) - amplitudes


def solution(mesh):
    placed = (P("up", "down"), P("up", "down"), P(), P(), P(), P(), P(), P())
    return jax.shard_map(
        body, mesh=mesh, in_specs=placed, out_specs=P("up", "down"), check_vma=False
    )
```

```python
import jax
import jax.numpy as jnp
from jax import lax
from jax.experimental import pallas as pl
from jax.experimental.pallas import tpu as pltpu
from jax.sharding import PartitionSpec as P

coupling = 0.5
center = 2.0
half_span = 2.0

LANES = 128


def block_order(block_cols, block_ids, shared_count):
    matched = block_ids[:, :, None] == jnp.arange(shared_count, dtype=jnp.int32)[None, None, :]
    return jnp.sum(jnp.where(matched, block_cols[:, :, None], 0), axis=1)


def _fill_rolled(src_ref, src2_ref):
    pairs = src_ref.shape[0]
    half = src_ref.shape[-1] // 2

    def one(i, carry):
        piece = src_ref[i]
        src2_ref[i] = piece
        src2_ref[pairs + i] = pltpu.roll(piece, half, 1)
        return carry

    lax.fori_loop(0, pairs, one, 0)


def _stage_row(idx_ref, base, src2_ref, stage_ref, row0, rows, shared_count, half):
    for t in range(shared_count // 2):
        even = idx_ref[base + 2 * t]
        odd = idx_ref[base + 2 * t + 1]
        stage_ref[row0:row0 + rows, t * LANES:t * LANES + half] = src2_ref[even, :, 0:half]
        stage_ref[row0:row0 + rows, t * LANES + half:(t + 1) * LANES] = src2_ref[odd, :, half:LANES]


def source_index(order, pairs):
    parity = jnp.arange(order.shape[-1], dtype=jnp.int32) % 2
    return ((order & 1) ^ parity) * pairs + (order >> 1)


def up_kernel(idx_ref, x_ref, w_ref, o_ref, src2_ref, stage_ref):
    pairs, n, _ = x_ref.shape
    block_width = w_ref.shape[1]
    shared_count = w_ref.shape[0] // block_width
    rows_per_chunk = stage_ref.shape[0] // n
    _fill_rolled(x_ref, src2_ref)

    def chunk(g, carry):
        for rr in range(rows_per_chunk):
            r = g * rows_per_chunk + rr
            _stage_row(idx_ref, r * shared_count, src2_ref, stage_ref, rr * n, n,
                       shared_count, block_width)
        res = jnp.dot(stage_ref[...], w_ref[...], preferred_element_type=jnp.float32)
        for rr in range(0, rows_per_chunk, 2):
            i = (g * rows_per_chunk + rr) // 2
            o_ref[i, :, 0:block_width] = res[rr * n:(rr + 1) * n]
            o_ref[i, :, block_width:2 * block_width] = res[(rr + 1) * n:(rr + 2) * n]
        return carry

    lax.fori_loop(0, 2 * pairs // rows_per_chunk, chunk, 0)


def down_kernel(idx_ref, g_ref, w_ref, o_ref, src_ref, w2_ref, stage_ref):
    sources, rows, cols = g_ref.shape
    block_width = w_ref.shape[1]
    shared_count = w_ref.shape[0] // block_width
    own_blocks = o_ref.shape[1] // block_width
    per_source = cols // LANES

    def relayout(i, carry):
        for m in range(per_source):
            src_ref[i * per_source + m] = g_ref[i, :, m * LANES:(m + 1) * LANES]
        return carry

    lax.fori_loop(0, sources, relayout, 0)
    for s in range(shared_count):
        block = w_ref[s * block_width:(s + 1) * block_width, :]
        w2_ref[s * LANES:s * LANES + block_width, :] = block
        w2_ref[s * LANES + block_width:(s + 1) * LANES, :] = block
    half_of_lane = jnp.where(
        lax.broadcasted_iota(jnp.int32, (rows, LANES), 1) >= block_width, 1, 0
    )
    for r in range(own_blocks):
        for s in range(shared_count):
            c = idx_ref[r * shared_count + s]
            piece = src_ref[lax.shift_right_logical(c, 1)]
            keep = half_of_lane == (c & 1)
            stage_ref[:, s * LANES:(s + 1) * LANES] = jnp.where(keep, piece, jnp.zeros_like(piece))
        o_ref[:, r * block_width:(r + 1) * block_width] = jnp.dot(
            stage_ref[...], w2_ref[...], preferred_element_type=jnp.float32
        )


def up_hop(idx, x, w):
    pairs, n, _ = x.shape
    rows_per_chunk = 8
    return pl.pallas_call(
        up_kernel,
        out_shape=jax.ShapeDtypeStruct((pairs, n, LANES), jnp.float32),
        in_specs=[
            pl.BlockSpec(memory_space=pltpu.SMEM),
            pl.BlockSpec(memory_space=pltpu.VMEM),
            pl.BlockSpec(memory_space=pltpu.VMEM),
        ],
        out_specs=pl.BlockSpec(memory_space=pltpu.VMEM),
        scratch_shapes=[
            pltpu.VMEM((2 * pairs, n, LANES), jnp.bfloat16),
            pltpu.VMEM((rows_per_chunk * n, w.shape[0]), jnp.bfloat16),
        ],
    )(idx, x, w)


def down_hop(idx, g, w, own_cols):
    _, rows, _ = g.shape
    return pl.pallas_call(
        down_kernel,
        out_shape=jax.ShapeDtypeStruct((rows, own_cols), jnp.float32),
        in_specs=[
            pl.BlockSpec(memory_space=pltpu.SMEM),
            pl.BlockSpec(memory_space=pltpu.VMEM),
            pl.BlockSpec(memory_space=pltpu.VMEM),
        ],
        out_specs=pl.BlockSpec(memory_space=pltpu.VMEM),
        scratch_shapes=[
            pltpu.VMEM((g.shape[0] * g.shape[2] // LANES, rows, LANES), jnp.bfloat16),
            pltpu.VMEM((2 * w.shape[0], w.shape[1]), jnp.bfloat16),
            pltpu.VMEM((rows, 2 * w.shape[0]), jnp.bfloat16),
        ],
    )(idx, g, w)


def body(amplitudes, double_occ, up_cols, up_ids, up_blocks, down_cols, down_ids, down_blocks):
    shared_count = up_blocks.shape[0]
    block_width = up_blocks.shape[1]
    local_rows, local_cols = amplitudes.shape
    up_count = lax.axis_size("up")
    own_blocks = local_cols // block_width
    up_idx = source_index(block_order(up_cols, up_ids, shared_count), up_count).reshape(-1)
    down_order = block_order(down_cols, down_ids, shared_count)
    down_idx = lax.dynamic_slice_in_dim(
        down_order, lax.axis_index("down") * own_blocks, own_blocks, 0
    ).reshape(-1)
    up_table = up_blocks.reshape(shared_count * block_width, block_width)
    down_table = down_blocks.reshape(shared_count * block_width, block_width)
    onsite = coupling * double_occ.astype(jnp.float32) - center
    col_chunk = local_cols // up_count

    def to_columns(values):
        return values.T.reshape(up_count, col_chunk, local_rows)

    def to_rows(pieces):
        return pieces.reshape(local_cols, local_rows).T

    def exchange_up(pieces):
        return lax.all_to_all(pieces, "up", 0, 0, tiled=True)

    def down_part(rounded):
        gathered = lax.all_gather(rounded, "down", axis=0)
        return down_hop(down_idx, gathered, down_table, local_cols)

    rounded0 = amplitudes.astype(jnp.bfloat16)
    up0_cols = up_hop(up_idx, exchange_up(to_columns(rounded0)), up_table)
    partial_rows = onsite * amplitudes + down_part(rounded0)
    both = exchange_up(jnp.concatenate([to_columns(partial_rows), up0_cols], axis=1))
    partial_cols = both[:, :col_chunk]
    up0_rows = to_rows(both[:, col_chunk:])
    first_cols = (partial_cols + up0_cols) / half_span
    first_rows = (partial_rows + up0_rows) / half_span

    up1_cols = up_hop(up_idx, first_cols.astype(jnp.bfloat16), up_table)
    down1_rows = down_part(first_rows.astype(jnp.bfloat16))
    up1_rows = to_rows(exchange_up(up1_cols))
    return 2.0 * ((onsite * first_rows + up1_rows + down1_rows) / half_span) - amplitudes


def solution(mesh):
    placed = (P("up", "down"), P("up", "down"), P(), P(), P(), P(), P(), P())
    return jax.shard_map(
        body, mesh=mesh, in_specs=placed, out_specs=P("up", "down"), check_vma=False
    )
```

```python
import jax
import jax.numpy as jnp
from jax import lax
from jax.experimental import pallas as pl
from jax.experimental.pallas import tpu as pltpu
from jax.sharding import PartitionSpec as P


coupling = 0.5
center = 2.0
half_span = 2.0

LANES = 128


def block_order(block_cols, block_ids, shared_count):
    matched = block_ids[:, :, None] == jnp.arange(shared_count, dtype=jnp.int32)[None, None, :]
    return jnp.sum(jnp.where(matched, block_cols[:, :, None], 0), axis=1)


def _fill_rolled(src_ref, src2_ref):
    pairs = src_ref.shape[0]
    half = src_ref.shape[-1] // 2

    def one(i, carry):
        piece = src_ref[i]
        src2_ref[i] = piece
        src2_ref[pairs + i] = pltpu.roll(piece, half, 1)
        return carry

    lax.fori_loop(0, pairs, one, 0)


def _stage_row(idx_ref, base, src2_ref, stage_ref, row0, rows, shared_count, half):
    for t in range(shared_count // 2):
        even = idx_ref[base + 2 * t]
        odd = idx_ref[base + 2 * t + 1]
        stage_ref[row0:row0 + rows, t * LANES:t * LANES + half] = src2_ref[even, :, 0:half]
        stage_ref[row0:row0 + rows, t * LANES + half:(t + 1) * LANES] = src2_ref[odd, :, half:LANES]


def source_index(order, pairs):
    parity = jnp.arange(order.shape[-1], dtype=jnp.int32) % 2
    return ((order & 1) ^ parity) * pairs + (order >> 1)


def up_kernel(idx_ref, x_ref, w_ref, o_ref, src2_ref, stage_ref):
    pairs, n, _ = x_ref.shape
    block_width = w_ref.shape[1]
    shared_count = w_ref.shape[0] // block_width
    rows_per_chunk = stage_ref.shape[0] // n
    _fill_rolled(x_ref, src2_ref)

    def chunk(g, carry):
        for rr in range(rows_per_chunk):
            r = g * rows_per_chunk + rr
            _stage_row(idx_ref, r * shared_count, src2_ref, stage_ref, rr * n, n,
                       shared_count, block_width)
        res = jnp.dot(stage_ref[...], w_ref[...], preferred_element_type=jnp.float32)
        for rr in range(0, rows_per_chunk, 2):
            i = (g * rows_per_chunk + rr) // 2
            o_ref[i, :, 0:block_width] = res[rr * n:(rr + 1) * n]
            o_ref[i, :, block_width:2 * block_width] = res[(rr + 1) * n:(rr + 2) * n]
        return carry

    lax.fori_loop(0, 2 * pairs // rows_per_chunk, chunk, 0)


def down_kernel(idx_ref, g_ref, w_ref, o_ref, src_ref, w2_ref, stage_ref):
    sources, rows, cols = g_ref.shape
    block_width = w_ref.shape[1]
    shared_count = w_ref.shape[0] // block_width
    own_blocks = o_ref.shape[1] // block_width
    per_source = cols // LANES

    def relayout(i, carry):
        for m in range(per_source):
            src_ref[i * per_source + m] = g_ref[i, :, m * LANES:(m + 1) * LANES]
        return carry

    lax.fori_loop(0, sources, relayout, 0)
    for s in range(shared_count):
        block = w_ref[s * block_width:(s + 1) * block_width, :]
        w2_ref[s * LANES:s * LANES + block_width, :] = block
        w2_ref[s * LANES + block_width:(s + 1) * LANES, :] = block
    half_of_lane = jnp.where(
        lax.broadcasted_iota(jnp.int32, (rows, LANES), 1) >= block_width, 1, 0
    )
    for r in range(own_blocks):
        for s in range(shared_count):
            c = idx_ref[r * shared_count + s]
            piece = src_ref[lax.shift_right_logical(c, 1)]
            keep = half_of_lane == (c & 1)
            stage_ref[:, s * LANES:(s + 1) * LANES] = jnp.where(keep, piece, jnp.zeros_like(piece))
        o_ref[:, r * block_width:(r + 1) * block_width] = jnp.dot(
            stage_ref[...], w2_ref[...], preferred_element_type=jnp.float32
        )


def up_hop(idx, x, w):
    pairs, n, _ = x.shape
    rows_per_chunk = 8
    return pl.pallas_call(
        up_kernel,
        out_shape=jax.ShapeDtypeStruct((pairs, n, LANES), jnp.float32),
        in_specs=[
            pl.BlockSpec(memory_space=pltpu.SMEM),
            pl.BlockSpec(memory_space=pltpu.VMEM),
            pl.BlockSpec(memory_space=pltpu.VMEM),
        ],
        out_specs=pl.BlockSpec(memory_space=pltpu.VMEM),
        scratch_shapes=[
            pltpu.VMEM((2 * pairs, n, LANES), jnp.bfloat16),
            pltpu.VMEM((rows_per_chunk * n, w.shape[0]), jnp.bfloat16),
        ],
    )(idx, x, w)


def down_hop(idx, g, w, own_cols):
    _, rows, _ = g.shape
    return pl.pallas_call(
        down_kernel,
        out_shape=jax.ShapeDtypeStruct((rows, own_cols), jnp.float32),
        in_specs=[
            pl.BlockSpec(memory_space=pltpu.SMEM),
            pl.BlockSpec(memory_space=pltpu.VMEM),
            pl.BlockSpec(memory_space=pltpu.VMEM),
        ],
        out_specs=pl.BlockSpec(memory_space=pltpu.VMEM),
        scratch_shapes=[
            pltpu.VMEM((g.shape[0] * g.shape[2] // LANES, rows, LANES), jnp.bfloat16),
            pltpu.VMEM((2 * w.shape[0], w.shape[1]), jnp.bfloat16),
            pltpu.VMEM((rows, 2 * w.shape[0]), jnp.bfloat16),
        ],
    )(idx, g, w)


def body(amplitudes, double_occ, up_cols, up_ids, up_blocks, down_cols, down_ids, down_blocks):
    shared_count = up_blocks.shape[0]
    block_width = up_blocks.shape[1]
    local_rows, local_cols = amplitudes.shape
    up_count = lax.axis_size("up")
    own_blocks = local_cols // block_width
    up_idx = source_index(block_order(up_cols, up_ids, shared_count), up_count).reshape(-1)
    down_order = block_order(down_cols, down_ids, shared_count)
    down_idx = lax.dynamic_slice_in_dim(
        down_order, lax.axis_index("down") * own_blocks, own_blocks, 0
    ).reshape(-1)
    up_table = up_blocks.reshape(shared_count * block_width, block_width)
    down_table = down_blocks.reshape(shared_count * block_width, block_width)
    onsite = coupling * double_occ.astype(jnp.float32) - center
    col_chunk = local_cols // up_count

    def to_columns(values):
        return values.T.reshape(up_count, col_chunk, local_rows)

    def to_rows(pieces):
        return pieces.reshape(local_cols, local_rows).T

    def exchange_up(pieces):
        return lax.all_to_all(pieces, "up", 0, 0, tiled=True)

    def down_part(rounded):
        copies = jnp.broadcast_to(rounded[None], (lax.axis_size("down"),) + rounded.shape)
        gathered = lax.all_to_all(copies, "down", 0, 0, tiled=True)
        return down_hop(down_idx, gathered, down_table, local_cols)

    rounded0 = amplitudes.astype(jnp.bfloat16)
    sent0 = exchange_up(to_columns(rounded0))
    up0_cols = up_hop(up_idx, sent0, up_table)
    partial_rows = onsite * amplitudes + down_part(rounded0)
    both = exchange_up(jnp.concatenate([to_columns(partial_rows), up0_cols], axis=1))
    partial_cols = both[:, :col_chunk]
    up0_rows = to_rows(both[:, col_chunk:])
    first_cols = (partial_cols + up0_cols) / half_span
    first_rows = (partial_rows + up0_rows) / half_span

    up1_cols = up_hop(up_idx, first_cols.astype(jnp.bfloat16), up_table)
    down1_rows = down_part(first_rows.astype(jnp.bfloat16))
    up1_rows = to_rows(exchange_up(up1_cols))
    return 2.0 * ((onsite * first_rows + up1_rows + down1_rows) / half_span) - amplitudes


def solution(mesh):
    placed = (P("up", "down"), P("up", "down"), P(), P(), P(), P(), P(), P())
    return jax.shard_map(
        body, mesh=mesh, in_specs=placed, out_specs=P("up", "down"), check_vma=False
    )
```

```python
import jax
import jax.numpy as jnp
from jax import lax
from jax.experimental import pallas as pl
from jax.experimental.pallas import tpu as pltpu
from jax.sharding import PartitionSpec as P


coupling = 0.5
center = 2.0
half_span = 2.0

LANES = 128


def block_order(block_cols, block_ids, shared_count):
    matched = block_ids[:, :, None] == jnp.arange(shared_count, dtype=jnp.int32)[None, None, :]
    return jnp.sum(jnp.where(matched, block_cols[:, :, None], 0), axis=1)


def _fill_rolled(src_ref, src2_ref):
    pairs = src_ref.shape[0]
    half = src_ref.shape[-1] // 2

    def one(i, carry):
        piece = src_ref[i]
        src2_ref[i] = piece
        src2_ref[pairs + i] = pltpu.roll(piece, half, 1)
        return carry

    lax.fori_loop(0, pairs, one, 0)


def _stage_row(idx_ref, base, src2_ref, stage_ref, row0, rows, shared_count, half):
    for t in range(shared_count // 2):
        even = idx_ref[base + 2 * t]
        odd = idx_ref[base + 2 * t + 1]
        stage_ref[row0:row0 + rows, t * LANES:t * LANES + half] = src2_ref[even, :, 0:half]
        stage_ref[row0:row0 + rows, t * LANES + half:(t + 1) * LANES] = src2_ref[odd, :, half:LANES]


def source_index(order, pairs):
    parity = jnp.arange(order.shape[-1], dtype=jnp.int32) % 2
    return ((order & 1) ^ parity) * pairs + (order >> 1)


def up_kernel(idx_ref, x_ref, w_ref, o_ref, src2_ref, stage_ref):
    pairs, n, _ = x_ref.shape
    block_width = w_ref.shape[1]
    shared_count = w_ref.shape[0] // block_width
    rows_per_chunk = stage_ref.shape[0] // n
    _fill_rolled(x_ref, src2_ref)

    def chunk(g, carry):
        for rr in range(rows_per_chunk):
            r = g * rows_per_chunk + rr
            _stage_row(idx_ref, r * shared_count, src2_ref, stage_ref, rr * n, n,
                       shared_count, block_width)
        res = jnp.dot(stage_ref[...], w_ref[...], preferred_element_type=jnp.float32)
        for rr in range(0, rows_per_chunk, 2):
            i = (g * rows_per_chunk + rr) // 2
            o_ref[i, :, 0:block_width] = res[rr * n:(rr + 1) * n]
            o_ref[i, :, block_width:2 * block_width] = res[(rr + 1) * n:(rr + 2) * n]
        return carry

    lax.fori_loop(0, 2 * pairs // rows_per_chunk, chunk, 0)


def down_kernel(idx_ref, g_ref, w_ref, o_ref, src_ref, w2_ref, stage_ref):
    sources, rows, cols = g_ref.shape
    block_width = w_ref.shape[1]
    shared_count = w_ref.shape[0] // block_width
    own_blocks = o_ref.shape[1] // block_width
    per_source = cols // LANES

    def relayout(i, carry):
        for m in range(per_source):
            src_ref[i * per_source + m] = g_ref[i, :, m * LANES:(m + 1) * LANES]
        return carry

    lax.fori_loop(0, sources, relayout, 0)
    for s in range(shared_count):
        block = w_ref[s * block_width:(s + 1) * block_width, :]
        w2_ref[s * LANES:s * LANES + block_width, :] = block
        w2_ref[s * LANES + block_width:(s + 1) * LANES, :] = block
    half_of_lane = jnp.where(
        lax.broadcasted_iota(jnp.int32, (rows, LANES), 1) >= block_width, 1, 0
    )
    for r in range(own_blocks):
        for s in range(shared_count):
            c = idx_ref[r * shared_count + s]
            piece = src_ref[lax.shift_right_logical(c, 1)]
            keep = half_of_lane == (c & 1)
            stage_ref[:, s * LANES:(s + 1) * LANES] = jnp.where(keep, piece, jnp.zeros_like(piece))
        o_ref[:, r * block_width:(r + 1) * block_width] = jnp.dot(
            stage_ref[...], w2_ref[...], preferred_element_type=jnp.float32
        )


def transpose_round_kernel(x_ref, o_ref):
    for m in range(x_ref.shape[1] // LANES):
        tile = x_ref[:, m * LANES:(m + 1) * LANES]
        o_ref[m * LANES:(m + 1) * LANES, :] = tile.T.astype(o_ref.dtype)


def transpose_round(x):
    rows, cols = x.shape
    return pl.pallas_call(
        transpose_round_kernel,
        out_shape=jax.ShapeDtypeStruct((cols, rows), jnp.bfloat16),
        in_specs=[pl.BlockSpec(memory_space=pltpu.VMEM)],
        out_specs=pl.BlockSpec(memory_space=pltpu.VMEM),
    )(x)


def up_hop(idx, x, w):
    pairs, n, _ = x.shape
    rows_per_chunk = 8
    return pl.pallas_call(
        up_kernel,
        out_shape=jax.ShapeDtypeStruct((pairs, n, LANES), jnp.float32),
        in_specs=[
            pl.BlockSpec(memory_space=pltpu.SMEM),
            pl.BlockSpec(memory_space=pltpu.VMEM),
            pl.BlockSpec(memory_space=pltpu.VMEM),
        ],
        out_specs=pl.BlockSpec(memory_space=pltpu.VMEM),
        scratch_shapes=[
            pltpu.VMEM((2 * pairs, n, LANES), jnp.bfloat16),
            pltpu.VMEM((rows_per_chunk * n, w.shape[0]), jnp.bfloat16),
        ],
    )(idx, x, w)


def down_hop(idx, g, w, own_cols):
    _, rows, _ = g.shape
    return pl.pallas_call(
        down_kernel,
        out_shape=jax.ShapeDtypeStruct((rows, own_cols), jnp.float32),
        in_specs=[
            pl.BlockSpec(memory_space=pltpu.SMEM),
            pl.BlockSpec(memory_space=pltpu.VMEM),
            pl.BlockSpec(memory_space=pltpu.VMEM),
        ],
        out_specs=pl.BlockSpec(memory_space=pltpu.VMEM),
        scratch_shapes=[
            pltpu.VMEM((g.shape[0] * g.shape[2] // LANES, rows, LANES), jnp.bfloat16),
            pltpu.VMEM((2 * w.shape[0], w.shape[1]), jnp.bfloat16),
            pltpu.VMEM((rows, 2 * w.shape[0]), jnp.bfloat16),
        ],
    )(idx, g, w)


def body(amplitudes, double_occ, up_cols, up_ids, up_blocks, down_cols, down_ids, down_blocks):
    shared_count = up_blocks.shape[0]
    block_width = up_blocks.shape[1]
    local_rows, local_cols = amplitudes.shape
    up_count = lax.axis_size("up")
    own_blocks = local_cols // block_width
    up_idx = source_index(block_order(up_cols, up_ids, shared_count), up_count).reshape(-1)
    down_order = block_order(down_cols, down_ids, shared_count)
    down_idx = lax.dynamic_slice_in_dim(
        down_order, lax.axis_index("down") * own_blocks, own_blocks, 0
    ).reshape(-1)
    up_table = up_blocks.reshape(shared_count * block_width, block_width)
    down_table = down_blocks.reshape(shared_count * block_width, block_width)
    onsite = coupling * double_occ.astype(jnp.float32) - center
    col_chunk = local_cols // up_count

    def to_columns(values):
        return values.T.reshape(up_count, col_chunk, local_rows)

    def to_rows(pieces):
        return pieces.reshape(local_cols, local_rows).T

    def exchange_up(pieces):
        return lax.all_to_all(pieces, "up", 0, 0, tiled=True)

    def down_part(rounded):
        copies = jnp.broadcast_to(rounded[None], (lax.axis_size("down"),) + rounded.shape)
        gathered = lax.all_to_all(copies, "down", 0, 0, tiled=True)
        return down_hop(down_idx, gathered, down_table, local_cols)

    rounded0 = amplitudes.astype(jnp.bfloat16)
    sent0 = exchange_up(
        transpose_round(amplitudes).reshape(up_count, col_chunk, local_rows)
    )
    up0_cols = up_hop(up_idx, sent0, up_table)
    partial_rows = onsite * amplitudes + down_part(rounded0)
    both = exchange_up(jnp.concatenate([to_columns(partial_rows), up0_cols], axis=1))
    partial_cols = both[:, :col_chunk]
    up0_rows = to_rows(both[:, col_chunk:])
    first_cols = (partial_cols + up0_cols) / half_span
    first_rows = (partial_rows + up0_rows) / half_span

    up1_cols = up_hop(up_idx, first_cols.astype(jnp.bfloat16), up_table)
    down1_rows = down_part(first_rows.astype(jnp.bfloat16))
    up1_rows = to_rows(exchange_up(up1_cols))
    return 2.0 * ((onsite * first_rows + up1_rows + down1_rows) / half_span) - amplitudes


def solution(mesh):
    placed = (P("up", "down"), P("up", "down"), P(), P(), P(), P(), P(), P())
    return jax.shard_map(
        body, mesh=mesh, in_specs=placed, out_specs=P("up", "down"), check_vma=False
    )
```

```python
import jax
import jax.numpy as jnp
from jax import lax
from jax.experimental import pallas as pl
from jax.experimental.pallas import tpu as pltpu
from jax.sharding import PartitionSpec as P


coupling = 0.5
center = 2.0
half_span = 2.0

LANES = 128


def block_order(block_cols, block_ids, shared_count):
    matched = block_ids[:, :, None] == jnp.arange(shared_count, dtype=jnp.int32)[None, None, :]
    return jnp.sum(jnp.where(matched, block_cols[:, :, None], 0), axis=1)


def _fill_rolled(src_ref, src2_ref):
    pairs = src_ref.shape[0]
    half = src_ref.shape[-1] // 2

    def one(i, carry):
        piece = src_ref[i]
        src2_ref[i] = piece
        src2_ref[pairs + i] = pltpu.roll(piece, half, 1)
        return carry

    lax.fori_loop(0, pairs, one, 0)


def _stage_row(idx_ref, base, src2_ref, stage_ref, row0, rows, shared_count, half):
    for t in range(shared_count // 2):
        even = idx_ref[base + 2 * t]
        odd = idx_ref[base + 2 * t + 1]
        stage_ref[row0:row0 + rows, t * LANES:t * LANES + half] = src2_ref[even, :, 0:half]
        stage_ref[row0:row0 + rows, t * LANES + half:(t + 1) * LANES] = src2_ref[odd, :, half:LANES]


def source_index(order, pairs):
    parity = jnp.arange(order.shape[-1], dtype=jnp.int32) % 2
    return ((order & 1) ^ parity) * pairs + (order >> 1)


def up_kernel(idx_ref, x_ref, w_ref, o_ref, src2_ref, stage_ref):
    pairs, n, _ = x_ref.shape
    block_width = w_ref.shape[1]
    shared_count = w_ref.shape[0] // block_width
    rows_per_chunk = stage_ref.shape[0] // n
    _fill_rolled(x_ref, src2_ref)

    def chunk(g, carry):
        for rr in range(rows_per_chunk):
            r = g * rows_per_chunk + rr
            _stage_row(idx_ref, r * shared_count, src2_ref, stage_ref, rr * n, n,
                       shared_count, block_width)
        res = jnp.dot(stage_ref[...], w_ref[...], preferred_element_type=jnp.float32)
        for rr in range(0, rows_per_chunk, 2):
            i = (g * rows_per_chunk + rr) // 2
            o_ref[i, :, 0:block_width] = res[rr * n:(rr + 1) * n]
            o_ref[i, :, block_width:2 * block_width] = res[(rr + 1) * n:(rr + 2) * n]
        return carry

    lax.fori_loop(0, 2 * pairs // rows_per_chunk, chunk, 0)


def dense_kernel(sid_ref, t_ref, m_ref):
    width = t_ref.shape[1]
    pairs = m_ref.shape[1] // LANES
    low_lanes = lax.broadcasted_iota(jnp.int32, (width, LANES), 1) < width

    def one(c, carry):
        for q in range(pairs):
            even = t_ref[sid_ref[c * 2 * pairs + 2 * q]]
            odd = t_ref[sid_ref[c * 2 * pairs + 2 * q + 1]]
            m_ref[pl.ds(pl.multiple_of(c * width, width), width), q * LANES:(q + 1) * LANES] = (
                jnp.where(low_lanes, even, odd)
            )
        return carry

    lax.fori_loop(0, m_ref.shape[0] // width, one, 0)


def dense_hop_kernel(g_ref, m_ref, o_ref):
    sources, _, cols = g_ref.shape
    acc = jnp.dot(g_ref[0], m_ref[0:cols, :], preferred_element_type=jnp.float32)
    for i in range(1, sources):
        acc = acc + jnp.dot(
            g_ref[i], m_ref[i * cols:(i + 1) * cols, :], preferred_element_type=jnp.float32
        )
    o_ref[...] = acc


def dense_table(sid, t2, strings, own_cols):
    return pl.pallas_call(
        dense_kernel,
        out_shape=jax.ShapeDtypeStruct((strings, own_cols), jnp.bfloat16),
        in_specs=[
            pl.BlockSpec(memory_space=pltpu.SMEM),
            pl.BlockSpec(memory_space=pltpu.VMEM),
        ],
        out_specs=pl.BlockSpec(memory_space=pltpu.VMEM),
    )(sid, t2)


def dense_hop(g, m):
    _, rows, _ = g.shape
    return pl.pallas_call(
        dense_hop_kernel,
        out_shape=jax.ShapeDtypeStruct((rows, m.shape[1]), jnp.float32),
        in_specs=[
            pl.BlockSpec(memory_space=pltpu.VMEM),
            pl.BlockSpec(memory_space=pltpu.VMEM),
        ],
        out_specs=pl.BlockSpec(memory_space=pltpu.VMEM),
    )(g, m)


def transpose_round_kernel(x_ref, o_ref):
    for m in range(x_ref.shape[1] // LANES):
        tile = x_ref[:, m * LANES:(m + 1) * LANES]
        o_ref[m * LANES:(m + 1) * LANES, :] = tile.T.astype(o_ref.dtype)


def transpose_round(x):
    rows, cols = x.shape
    return pl.pallas_call(
        transpose_round_kernel,
        out_shape=jax.ShapeDtypeStruct((cols, rows), jnp.bfloat16),
        in_specs=[pl.BlockSpec(memory_space=pltpu.VMEM)],
        out_specs=pl.BlockSpec(memory_space=pltpu.VMEM),
    )(x)


def up_hop(idx, x, w):
    pairs, n, _ = x.shape
    rows_per_chunk = 8
    return pl.pallas_call(
        up_kernel,
        out_shape=jax.ShapeDtypeStruct((pairs, n, LANES), jnp.float32),
        in_specs=[
            pl.BlockSpec(memory_space=pltpu.SMEM),
            pl.BlockSpec(memory_space=pltpu.VMEM),
            pl.BlockSpec(memory_space=pltpu.VMEM),
        ],
        out_specs=pl.BlockSpec(memory_space=pltpu.VMEM),
        scratch_shapes=[
            pltpu.VMEM((2 * pairs, n, LANES), jnp.bfloat16),
            pltpu.VMEM((rows_per_chunk * n, w.shape[0]), jnp.bfloat16),
        ],
    )(idx, x, w)


def body(amplitudes, double_occ, up_cols, up_ids, up_blocks, down_cols, down_ids, down_blocks):
    shared_count = up_blocks.shape[0]
    block_width = up_blocks.shape[1]
    local_rows, local_cols = amplitudes.shape
    up_count = lax.axis_size("up")
    own_blocks = local_cols // block_width
    up_idx = source_index(block_order(up_cols, up_ids, shared_count), up_count).reshape(-1)
    down_order = block_order(down_cols, down_ids, shared_count)
    down_idx = lax.dynamic_slice_in_dim(
        down_order, lax.axis_index("down") * own_blocks, own_blocks, 0
    ).reshape(-1)
    up_table = up_blocks.reshape(shared_count * block_width, block_width)
    onsite = coupling * double_occ.astype(jnp.float32) - center
    col_chunk = local_cols // up_count

    def to_columns(values):
        return values.T.reshape(up_count, col_chunk, local_rows)

    def to_rows(pieces):
        return pieces.reshape(local_cols, local_rows).T

    def exchange_up(pieces):
        return lax.all_to_all(pieces, "up", 0, 0, tiled=True)

    def down_part(rounded):
        copies = jnp.broadcast_to(rounded[None], (lax.axis_size("down"),) + rounded.shape)
        gathered = lax.all_to_all(copies, "down", 0, 0, tiled=True)
        return dense_hop(gathered, down_dense)

    rounded0 = amplitudes.astype(jnp.bfloat16)
    own_order = down_idx.reshape(own_blocks, shared_count)
    block_ids = jnp.arange(lax.axis_size("down") * own_blocks, dtype=jnp.int32)
    hit = own_order[None, :, :] == block_ids[:, None, None]
    slot = jnp.sum(jnp.where(hit, jnp.arange(shared_count, dtype=jnp.int32) + 1, 0), axis=2)
    sid = jnp.where(slot == 0, shared_count, slot - 1).reshape(-1)
    padded = jnp.concatenate([down_blocks, jnp.zeros_like(down_blocks[:1])], axis=0)
    down_dense = dense_table(
        sid, jnp.concatenate([padded, padded], axis=2),
        lax.axis_size("down") * local_cols, local_cols,
    )
    sent0 = exchange_up(
        transpose_round(amplitudes).reshape(up_count, col_chunk, local_rows)
    )
    up0_cols = up_hop(up_idx, sent0, up_table)
    partial_rows = onsite * amplitudes + down_part(rounded0)
    both = exchange_up(jnp.concatenate([to_columns(partial_rows), up0_cols], axis=1))
    partial_cols = both[:, :col_chunk]
    up0_rows = to_rows(both[:, col_chunk:])
    first_cols = (partial_cols + up0_cols) / half_span
    first_rows = (partial_rows + up0_rows) / half_span

    up1_cols = up_hop(up_idx, first_cols.astype(jnp.bfloat16), up_table)
    down1_rows = down_part(first_rows.astype(jnp.bfloat16))
    up1_rows = to_rows(exchange_up(up1_cols))
    return 2.0 * ((onsite * first_rows + up1_rows + down1_rows) / half_span) - amplitudes


def solution(mesh):
    placed = (P("up", "down"), P("up", "down"), P(), P(), P(), P(), P(), P())
    return jax.shard_map(
        body, mesh=mesh, in_specs=placed, out_specs=P("up", "down"), check_vma=False
    )
```

```python
import jax
import jax.numpy as jnp
from jax import lax
from jax.experimental import pallas as pl
from jax.experimental.pallas import tpu as pltpu
from jax.sharding import PartitionSpec as P


coupling = 0.5
center = 2.0
half_span = 2.0

LANES = 128


def block_order(block_cols, block_ids, shared_count):
    matched = block_ids[:, :, None] == jnp.arange(shared_count, dtype=jnp.int32)[None, None, :]
    return jnp.sum(jnp.where(matched, block_cols[:, :, None], 0), axis=1)


def _fill_rolled(src_ref, src2_ref):
    pairs = src_ref.shape[0]
    half = src_ref.shape[-1] // 2

    def one(i, carry):
        piece = src_ref[i]
        src2_ref[i] = piece
        src2_ref[pairs + i] = pltpu.roll(piece, half, 1)
        return carry

    lax.fori_loop(0, pairs, one, 0)


def _stage_row(idx_ref, base, src2_ref, stage_ref, row0, rows, shared_count, half):
    for t in range(shared_count // 2):
        even = idx_ref[base + 2 * t]
        odd = idx_ref[base + 2 * t + 1]
        stage_ref[row0:row0 + rows, t * LANES:t * LANES + half] = src2_ref[even, :, 0:half]
        stage_ref[row0:row0 + rows, t * LANES + half:(t + 1) * LANES] = src2_ref[odd, :, half:LANES]


def source_index(order, pairs):
    parity = jnp.arange(order.shape[-1], dtype=jnp.int32) % 2
    return ((order & 1) ^ parity) * pairs + (order >> 1)


def up_kernel(idx_ref, x_ref, w_ref, o_ref, src2_ref, stage_ref):
    pairs, n, _ = x_ref.shape
    block_width = w_ref.shape[1]
    shared_count = w_ref.shape[0] // block_width
    rows_per_chunk = stage_ref.shape[0] // n
    _fill_rolled(x_ref, src2_ref)

    def chunk(g, carry):
        for rr in range(rows_per_chunk):
            r = g * rows_per_chunk + rr
            _stage_row(idx_ref, r * shared_count, src2_ref, stage_ref, rr * n, n,
                       shared_count, block_width)
        res = jnp.dot(stage_ref[...], w_ref[...], preferred_element_type=jnp.float32)
        for rr in range(0, rows_per_chunk, 2):
            i = (g * rows_per_chunk + rr) // 2
            o_ref[i, :, 0:block_width] = res[rr * n:(rr + 1) * n]
            o_ref[i, :, block_width:2 * block_width] = res[(rr + 1) * n:(rr + 2) * n]
        return carry

    lax.fori_loop(0, 2 * pairs // rows_per_chunk, chunk, 0)


def dense_kernel(own_ref, blocks_ref, m_ref, sid_ref, t_ref):
    shared_count, width, _ = blocks_ref.shape
    own_blocks = m_ref.shape[1] // width
    pairs = own_blocks // 2

    def clear(i, carry):
        sid_ref[i] = shared_count
        return carry

    lax.fori_loop(0, sid_ref.shape[0], clear, 0)

    def scatter(k, carry):
        r = k // shared_count
        sid_ref[own_ref[k] * own_blocks + r] = k % shared_count
        return carry

    lax.fori_loop(0, own_blocks * shared_count, scatter, 0)
    for s in range(shared_count):
        block = blocks_ref[s]
        t_ref[s, :, 0:width] = block
        t_ref[s, :, width:2 * width] = block
    t_ref[shared_count] = jnp.zeros(t_ref.shape[1:], t_ref.dtype)
    low_lanes = lax.broadcasted_iota(jnp.int32, (width, LANES), 1) < width

    def one(c, carry):
        for q in range(pairs):
            even = t_ref[sid_ref[c * own_blocks + 2 * q]]
            odd = t_ref[sid_ref[c * own_blocks + 2 * q + 1]]
            m_ref[pl.ds(pl.multiple_of(c * width, width), width), q * LANES:(q + 1) * LANES] = (
                jnp.where(low_lanes, even, odd)
            )
        return carry

    lax.fori_loop(0, m_ref.shape[0] // width, one, 0)


def dense_hop_kernel(g_ref, m_ref, o_ref):
    sources, _, cols = g_ref.shape
    acc = jnp.dot(g_ref[0], m_ref[0:cols, :], preferred_element_type=jnp.float32)
    for i in range(1, sources):
        acc = acc + jnp.dot(
            g_ref[i], m_ref[i * cols:(i + 1) * cols, :], preferred_element_type=jnp.float32
        )
    o_ref[...] = acc


def dense_table(own_order, blocks, strings, own_cols):
    shared_count, width, _ = blocks.shape
    return pl.pallas_call(
        dense_kernel,
        out_shape=jax.ShapeDtypeStruct((strings, own_cols), jnp.bfloat16),
        in_specs=[
            pl.BlockSpec(memory_space=pltpu.SMEM),
            pl.BlockSpec(memory_space=pltpu.VMEM),
        ],
        out_specs=pl.BlockSpec(memory_space=pltpu.VMEM),
        scratch_shapes=[
            pltpu.SMEM(((strings // width) * (own_cols // width),), jnp.int32),
            pltpu.VMEM((shared_count + 1, width, 2 * width), blocks.dtype),
        ],
    )(own_order, blocks)


def dense_hop(g, m):
    _, rows, _ = g.shape
    return pl.pallas_call(
        dense_hop_kernel,
        out_shape=jax.ShapeDtypeStruct((rows, m.shape[1]), jnp.float32),
        in_specs=[
            pl.BlockSpec(memory_space=pltpu.VMEM),
            pl.BlockSpec(memory_space=pltpu.VMEM),
        ],
        out_specs=pl.BlockSpec(memory_space=pltpu.VMEM),
    )(g, m)


def transpose_round_kernel(x_ref, o_ref):
    for m in range(x_ref.shape[1] // LANES):
        tile = x_ref[:, m * LANES:(m + 1) * LANES]
        o_ref[m * LANES:(m + 1) * LANES, :] = tile.T.astype(o_ref.dtype)


def transpose_round(x):
    rows, cols = x.shape
    return pl.pallas_call(
        transpose_round_kernel,
        out_shape=jax.ShapeDtypeStruct((cols, rows), jnp.bfloat16),
        in_specs=[pl.BlockSpec(memory_space=pltpu.VMEM)],
        out_specs=pl.BlockSpec(memory_space=pltpu.VMEM),
    )(x)


def up_hop(idx, x, w):
    pairs, n, _ = x.shape
    rows_per_chunk = 8
    return pl.pallas_call(
        up_kernel,
        out_shape=jax.ShapeDtypeStruct((pairs, n, LANES), jnp.float32),
        in_specs=[
            pl.BlockSpec(memory_space=pltpu.SMEM),
            pl.BlockSpec(memory_space=pltpu.VMEM),
            pl.BlockSpec(memory_space=pltpu.VMEM),
        ],
        out_specs=pl.BlockSpec(memory_space=pltpu.VMEM),
        scratch_shapes=[
            pltpu.VMEM((2 * pairs, n, LANES), jnp.bfloat16),
            pltpu.VMEM((rows_per_chunk * n, w.shape[0]), jnp.bfloat16),
        ],
    )(idx, x, w)


def body(amplitudes, double_occ, up_cols, up_ids, up_blocks, down_cols, down_ids, down_blocks):
    shared_count = up_blocks.shape[0]
    block_width = up_blocks.shape[1]
    local_rows, local_cols = amplitudes.shape
    up_count = lax.axis_size("up")
    own_blocks = local_cols // block_width
    up_idx = source_index(block_order(up_cols, up_ids, shared_count), up_count).reshape(-1)
    down_order = block_order(down_cols, down_ids, shared_count)
    down_idx = lax.dynamic_slice_in_dim(
        down_order, lax.axis_index("down") * own_blocks, own_blocks, 0
    ).reshape(-1)
    up_table = up_blocks.reshape(shared_count * block_width, block_width)
    onsite = coupling * double_occ.astype(jnp.float32) - center
    col_chunk = local_cols // up_count

    def to_columns(values):
        return values.T.reshape(up_count, col_chunk, local_rows)

    def to_rows(pieces):
        return pieces.reshape(local_cols, local_rows).T

    def exchange_up(pieces):
        return lax.all_to_all(pieces, "up", 0, 0, tiled=True)

    def down_part(rounded):
        copies = jnp.broadcast_to(rounded[None], (lax.axis_size("down"),) + rounded.shape)
        gathered = lax.all_to_all(copies, "down", 0, 0, tiled=True)
        return dense_hop(gathered, down_dense)

    rounded0 = amplitudes.astype(jnp.bfloat16)
    down_dense = dense_table(down_idx, down_blocks, lax.axis_size("down") * local_cols, local_cols)
    sent0 = exchange_up(
        transpose_round(amplitudes).reshape(up_count, col_chunk, local_rows)
    )
    up0_cols = up_hop(up_idx, sent0, up_table)
    partial_rows = onsite * amplitudes + down_part(rounded0)
    both = exchange_up(jnp.concatenate([to_columns(partial_rows), up0_cols], axis=1))
    partial_cols = both[:, :col_chunk]
    up0_rows = to_rows(both[:, col_chunk:])
    first_cols = (partial_cols + up0_cols) / half_span
    first_rows = (partial_rows + up0_rows) / half_span

    up1_cols = up_hop(up_idx, first_cols.astype(jnp.bfloat16), up_table)
    down1_rows = down_part(first_rows.astype(jnp.bfloat16))
    up1_rows = to_rows(exchange_up(up1_cols))
    return 2.0 * ((onsite * first_rows + up1_rows + down1_rows) / half_span) - amplitudes


def solution(mesh):
    placed = (P("up", "down"), P("up", "down"), P(), P(), P(), P(), P(), P())
    return jax.shard_map(
        body, mesh=mesh, in_specs=placed, out_specs=P("up", "down"), check_vma=False
    )
```

```python
import jax
import jax.numpy as jnp
from jax import lax
from jax.experimental import pallas as pl
from jax.experimental.pallas import tpu as pltpu
from jax.sharding import PartitionSpec as P


coupling = 0.5
center = 2.0
half_span = 2.0

LANES = 128


def block_order(block_cols, block_ids, shared_count):
    matched = block_ids[:, :, None] == jnp.arange(shared_count, dtype=jnp.int32)[None, None, :]
    return jnp.sum(jnp.where(matched, block_cols[:, :, None], 0), axis=1)


def _fill_rolled(src_ref, src2_ref):
    pairs = src_ref.shape[0]
    half = src_ref.shape[-1] // 2

    def one(i, carry):
        piece = src_ref[i]
        src2_ref[i] = piece
        src2_ref[pairs + i] = pltpu.roll(piece, half, 1)
        return carry

    lax.fori_loop(0, pairs, one, 0)


def _stage_row(idx_ref, base, src2_ref, stage_ref, row0, rows, shared_count, half):
    for t in range(shared_count // 2):
        even = idx_ref[base + 2 * t]
        odd = idx_ref[base + 2 * t + 1]
        stage_ref[row0:row0 + rows, t * LANES:t * LANES + half] = src2_ref[even, :, 0:half]
        stage_ref[row0:row0 + rows, t * LANES + half:(t + 1) * LANES] = src2_ref[odd, :, half:LANES]


def source_index(order, pairs):
    parity = jnp.arange(order.shape[-1], dtype=jnp.int32) % 2
    return ((order & 1) ^ parity) * pairs + (order >> 1)


def up_kernel(idx_ref, x_ref, w_ref, o_ref, src2_ref, stage_ref):
    pairs, n, _ = x_ref.shape
    block_width = w_ref.shape[1]
    shared_count = w_ref.shape[0] // block_width
    rows_per_chunk = stage_ref.shape[0] // n
    _fill_rolled(x_ref, src2_ref)

    def chunk(g, carry):
        for rr in range(rows_per_chunk):
            r = g * rows_per_chunk + rr
            _stage_row(idx_ref, r * shared_count, src2_ref, stage_ref, rr * n, n,
                       shared_count, block_width)
        res = jnp.dot(stage_ref[...], w_ref[...], preferred_element_type=jnp.float32)
        for rr in range(0, rows_per_chunk, 2):
            i = (g * rows_per_chunk + rr) // 2
            o_ref[i, :, 0:block_width] = res[rr * n:(rr + 1) * n]
            o_ref[i, :, block_width:2 * block_width] = res[(rr + 1) * n:(rr + 2) * n]
        return carry

    lax.fori_loop(0, 2 * pairs // rows_per_chunk, chunk, 0)


def down_kernel(idx_ref, g_ref, w_ref, a_ref, b_ref, o_ref, src_ref, w2_ref, stage_ref):
    sources, rows, cols = g_ref.shape
    block_width = w_ref.shape[1]
    shared_count = w_ref.shape[0] // block_width
    own_blocks = o_ref.shape[1] // block_width
    per_source = cols // LANES

    def relayout(i, carry):
        for m in range(per_source):
            src_ref[i * per_source + m] = g_ref[i, :, m * LANES:(m + 1) * LANES]
        return carry

    lax.fori_loop(0, sources, relayout, 0)
    for s in range(shared_count):
        block = w_ref[s * block_width:(s + 1) * block_width, :]
        w2_ref[s * LANES:s * LANES + block_width, :] = block
        w2_ref[s * LANES + block_width:(s + 1) * LANES, :] = block
    half_of_lane = jnp.where(
        lax.broadcasted_iota(jnp.int32, (rows, LANES), 1) >= block_width, 1, 0
    )
    for r in range(own_blocks):
        for s in range(shared_count):
            c = idx_ref[r * shared_count + s]
            piece = src_ref[lax.shift_right_logical(c, 1)]
            keep = half_of_lane == (c & 1)
            stage_ref[:, s * LANES:(s + 1) * LANES] = jnp.where(keep, piece, jnp.zeros_like(piece))
        cols_r = slice(r * block_width, (r + 1) * block_width)
        o_ref[:, cols_r] = a_ref[:, cols_r] * b_ref[:, cols_r] + jnp.dot(
            stage_ref[...], w2_ref[...], preferred_element_type=jnp.float32
        )


def transpose_round_kernel(x_ref, o_ref):
    for m in range(x_ref.shape[1] // LANES):
        tile = x_ref[:, m * LANES:(m + 1) * LANES]
        o_ref[m * LANES:(m + 1) * LANES, :] = tile.T.astype(o_ref.dtype)


def transpose_round(x):
    rows, cols = x.shape
    return pl.pallas_call(
        transpose_round_kernel,
        out_shape=jax.ShapeDtypeStruct((cols, rows), jnp.bfloat16),
        in_specs=[pl.BlockSpec(memory_space=pltpu.VMEM)],
        out_specs=pl.BlockSpec(memory_space=pltpu.VMEM),
    )(x)


def up_hop(idx, x, w):
    pairs, n, _ = x.shape
    rows_per_chunk = 8
    return pl.pallas_call(
        up_kernel,
        out_shape=jax.ShapeDtypeStruct((pairs, n, LANES), jnp.float32),
        in_specs=[
            pl.BlockSpec(memory_space=pltpu.SMEM),
            pl.BlockSpec(memory_space=pltpu.VMEM),
            pl.BlockSpec(memory_space=pltpu.VMEM),
        ],
        out_specs=pl.BlockSpec(memory_space=pltpu.VMEM),
        scratch_shapes=[
            pltpu.VMEM((2 * pairs, n, LANES), jnp.bfloat16),
            pltpu.VMEM((rows_per_chunk * n, w.shape[0]), jnp.bfloat16),
        ],
    )(idx, x, w)


def down_hop(idx, g, w, a, b):
    _, rows, _ = g.shape
    return pl.pallas_call(
        down_kernel,
        out_shape=jax.ShapeDtypeStruct(a.shape, jnp.float32),
        in_specs=[
            pl.BlockSpec(memory_space=pltpu.SMEM),
            pl.BlockSpec(memory_space=pltpu.VMEM),
            pl.BlockSpec(memory_space=pltpu.VMEM),
            pl.BlockSpec(memory_space=pltpu.VMEM),
            pl.BlockSpec(memory_space=pltpu.VMEM),
        ],
        out_specs=pl.BlockSpec(memory_space=pltpu.VMEM),
        scratch_shapes=[
            pltpu.VMEM((g.shape[0] * g.shape[2] // LANES, rows, LANES), jnp.bfloat16),
            pltpu.VMEM((2 * w.shape[0], w.shape[1]), jnp.bfloat16),
            pltpu.VMEM((rows, 2 * w.shape[0]), jnp.bfloat16),
        ],
    )(idx, g, w, a, b)


def body(amplitudes, double_occ, up_cols, up_ids, up_blocks, down_cols, down_ids, down_blocks):
    shared_count = up_blocks.shape[0]
    block_width = up_blocks.shape[1]
    local_rows, local_cols = amplitudes.shape
    up_count = lax.axis_size("up")
    own_blocks = local_cols // block_width
    up_idx = source_index(block_order(up_cols, up_ids, shared_count), up_count).reshape(-1)
    down_order = block_order(down_cols, down_ids, shared_count)
    down_idx = lax.dynamic_slice_in_dim(
        down_order, lax.axis_index("down") * own_blocks, own_blocks, 0
    ).reshape(-1)
    up_table = up_blocks.reshape(shared_count * block_width, block_width)
    down_table = down_blocks.reshape(shared_count * block_width, block_width)
    onsite = coupling * double_occ.astype(jnp.float32) - center
    col_chunk = local_cols // up_count

    def to_columns(values):
        return values.T.reshape(up_count, col_chunk, local_rows)

    def to_rows(pieces):
        return pieces.reshape(local_cols, local_rows).T

    def exchange_up(pieces):
        return lax.all_to_all(pieces, "up", 0, 0, tiled=True)

    def down_part(current, rounded):
        copies = jnp.broadcast_to(rounded[None], (lax.axis_size("down"),) + rounded.shape)
        gathered = lax.all_to_all(copies, "down", 0, 0, tiled=True)
        return down_hop(down_idx, gathered, down_table, onsite, current)

    rounded0 = amplitudes.astype(jnp.bfloat16)
    sent0 = exchange_up(
        transpose_round(amplitudes).reshape(up_count, col_chunk, local_rows)
    )
    up0_cols = up_hop(up_idx, sent0, up_table)
    partial_rows = down_part(amplitudes, rounded0)
    both = exchange_up(jnp.concatenate([to_columns(partial_rows), up0_cols], axis=1))
    partial_cols = both[:, :col_chunk]
    up0_rows = to_rows(both[:, col_chunk:])
    first_cols = (partial_cols + up0_cols) / half_span
    first_rows = (partial_rows + up0_rows) / half_span

    up1_cols = up_hop(up_idx, first_cols.astype(jnp.bfloat16), up_table)
    known_rows = down_part(first_rows, first_rows.astype(jnp.bfloat16))
    up1_rows = to_rows(exchange_up(up1_cols))
    return 2.0 * ((known_rows + up1_rows) / half_span) - amplitudes


def solution(mesh):
    placed = (P("up", "down"), P("up", "down"), P(), P(), P(), P(), P(), P())
    return jax.shard_map(
        body, mesh=mesh, in_specs=placed, out_specs=P("up", "down"), check_vma=False
    )
```

```python
import jax
import jax.numpy as jnp
from jax import lax
from jax.experimental import pallas as pl
from jax.experimental.pallas import tpu as pltpu
from jax.sharding import PartitionSpec as P


coupling = 0.5
center = 2.0
half_span = 2.0

LANES = 128


def block_order(block_cols, block_ids, shared_count):
    matched = block_ids[:, :, None] == jnp.arange(shared_count, dtype=jnp.int32)[None, None, :]
    return jnp.sum(jnp.where(matched, block_cols[:, :, None], 0), axis=1)


def _fill_rolled(load, pairs, src2_ref):
    half = src2_ref.shape[-1] // 2

    def one(i, carry):
        piece = load(i)
        src2_ref[i] = piece
        src2_ref[pairs + i] = pltpu.roll(piece, half, 1)
        return carry

    lax.fori_loop(0, pairs, one, 0)


def _stage_row(idx_ref, base, src2_ref, stage_ref, row0, rows, shared_count, half):
    for t in range(shared_count // 2):
        even = idx_ref[base + 2 * t]
        odd = idx_ref[base + 2 * t + 1]
        stage_ref[row0:row0 + rows, t * LANES:t * LANES + half] = src2_ref[even, :, 0:half]
        stage_ref[row0:row0 + rows, t * LANES + half:(t + 1) * LANES] = src2_ref[odd, :, half:LANES]


def source_index(order, pairs):
    parity = jnp.arange(order.shape[-1], dtype=jnp.int32) % 2
    return ((order & 1) ^ parity) * pairs + (order >> 1)


def up_kernel(idx_ref, x_ref, w_ref, o_ref, src2_ref, stage_ref):
    _fill_rolled(lambda i: x_ref[i], x_ref.shape[0], src2_ref)
    _up_body(idx_ref, w_ref, o_ref, src2_ref, stage_ref)


def up_kernel_halved(idx_ref, p_ref, u_ref, w_ref, o_ref, src2_ref, stage_ref):
    _fill_rolled(
        lambda i: ((p_ref[i] + u_ref[i]) / half_span).astype(jnp.bfloat16),
        p_ref.shape[0], src2_ref,
    )
    _up_body(idx_ref, w_ref, o_ref, src2_ref, stage_ref)


def _up_body(idx_ref, w_ref, o_ref, src2_ref, stage_ref):
    pairs, n, _ = o_ref.shape
    block_width = w_ref.shape[1]
    shared_count = w_ref.shape[0] // block_width
    rows_per_chunk = stage_ref.shape[0] // n

    def chunk(g, carry):
        for rr in range(rows_per_chunk):
            r = g * rows_per_chunk + rr
            _stage_row(idx_ref, r * shared_count, src2_ref, stage_ref, rr * n, n,
                       shared_count, block_width)
        res = jnp.dot(stage_ref[...], w_ref[...], preferred_element_type=jnp.float32)
        for rr in range(0, rows_per_chunk, 2):
            i = (g * rows_per_chunk + rr) // 2
            o_ref[i, :, 0:block_width] = res[rr * n:(rr + 1) * n]
            o_ref[i, :, block_width:2 * block_width] = res[(rr + 1) * n:(rr + 2) * n]
        return carry

    lax.fori_loop(0, 2 * pairs // rows_per_chunk, chunk, 0)


def down_kernel(idx_ref, g_ref, w_ref, o_ref, src_ref, w2_ref, stage_ref):
    sources, rows, cols = g_ref.shape
    block_width = w_ref.shape[1]
    shared_count = w_ref.shape[0] // block_width
    own_blocks = o_ref.shape[1] // block_width
    per_source = cols // LANES

    def relayout(i, carry):
        for m in range(per_source):
            src_ref[i * per_source + m] = g_ref[i, :, m * LANES:(m + 1) * LANES]
        return carry

    lax.fori_loop(0, sources, relayout, 0)
    for s in range(shared_count):
        block = w_ref[s * block_width:(s + 1) * block_width, :]
        w2_ref[s * LANES:s * LANES + block_width, :] = block
        w2_ref[s * LANES + block_width:(s + 1) * LANES, :] = block
    half_of_lane = jnp.where(
        lax.broadcasted_iota(jnp.int32, (rows, LANES), 1) >= block_width, 1, 0
    )
    for r in range(own_blocks):
        for s in range(shared_count):
            c = idx_ref[r * shared_count + s]
            piece = src_ref[lax.shift_right_logical(c, 1)]
            keep = half_of_lane == (c & 1)
            stage_ref[:, s * LANES:(s + 1) * LANES] = jnp.where(keep, piece, jnp.zeros_like(piece))
        o_ref[:, r * block_width:(r + 1) * block_width] = jnp.dot(
            stage_ref[...], w2_ref[...], preferred_element_type=jnp.float32
        )


def transpose_round_kernel(x_ref, o_ref):
    for m in range(x_ref.shape[1] // LANES):
        tile = x_ref[:, m * LANES:(m + 1) * LANES]
        o_ref[m * LANES:(m + 1) * LANES, :] = tile.T.astype(o_ref.dtype)


def transpose_round(x):
    rows, cols = x.shape
    return pl.pallas_call(
        transpose_round_kernel,
        out_shape=jax.ShapeDtypeStruct((cols, rows), jnp.bfloat16),
        in_specs=[pl.BlockSpec(memory_space=pltpu.VMEM)],
        out_specs=pl.BlockSpec(memory_space=pltpu.VMEM),
    )(x)


def up_hop(idx, w, *parts):
    pairs, n, _ = parts[0].shape
    rows_per_chunk = 8
    return pl.pallas_call(
        up_kernel if len(parts) == 1 else up_kernel_halved,
        out_shape=jax.ShapeDtypeStruct((pairs, n, LANES), jnp.float32),
        in_specs=[pl.BlockSpec(memory_space=pltpu.SMEM)]
        + [pl.BlockSpec(memory_space=pltpu.VMEM)] * (len(parts) + 1),
        out_specs=pl.BlockSpec(memory_space=pltpu.VMEM),
        scratch_shapes=[
            pltpu.VMEM((2 * pairs, n, LANES), jnp.bfloat16),
            pltpu.VMEM((rows_per_chunk * n, w.shape[0]), jnp.bfloat16),
        ],
    )(idx, *parts, w)


def down_hop(idx, g, w, own_cols):
    _, rows, _ = g.shape
    return pl.pallas_call(
        down_kernel,
        out_shape=jax.ShapeDtypeStruct((rows, own_cols), jnp.float32),
        in_specs=[
            pl.BlockSpec(memory_space=pltpu.SMEM),
            pl.BlockSpec(memory_space=pltpu.VMEM),
            pl.BlockSpec(memory_space=pltpu.VMEM),
        ],
        out_specs=pl.BlockSpec(memory_space=pltpu.VMEM),
        scratch_shapes=[
            pltpu.VMEM((g.shape[0] * g.shape[2] // LANES, rows, LANES), jnp.bfloat16),
            pltpu.VMEM((2 * w.shape[0], w.shape[1]), jnp.bfloat16),
            pltpu.VMEM((rows, 2 * w.shape[0]), jnp.bfloat16),
        ],
    )(idx, g, w)


def body(amplitudes, double_occ, up_cols, up_ids, up_blocks, down_cols, down_ids, down_blocks):
    shared_count = up_blocks.shape[0]
    block_width = up_blocks.shape[1]
    local_rows, local_cols = amplitudes.shape
    up_count = lax.axis_size("up")
    own_blocks = local_cols // block_width
    up_idx = source_index(block_order(up_cols, up_ids, shared_count), up_count).reshape(-1)
    down_order = block_order(down_cols, down_ids, shared_count)
    down_idx = lax.dynamic_slice_in_dim(
        down_order, lax.axis_index("down") * own_blocks, own_blocks, 0
    ).reshape(-1)
    up_table = up_blocks.reshape(shared_count * block_width, block_width)
    down_table = down_blocks.reshape(shared_count * block_width, block_width)
    onsite = coupling * double_occ.astype(jnp.float32) - center
    col_chunk = local_cols // up_count

    def to_columns(values):
        return values.T.reshape(up_count, col_chunk, local_rows)

    def to_rows(pieces):
        return pieces.reshape(local_cols, local_rows).T

    def exchange_up(pieces):
        return lax.all_to_all(pieces, "up", 0, 0, tiled=True)

    def down_part(rounded):
        copies = jnp.broadcast_to(rounded[None], (lax.axis_size("down"),) + rounded.shape)
        gathered = lax.all_to_all(copies, "down", 0, 0, tiled=True)
        return down_hop(down_idx, gathered, down_table, local_cols)

    rounded0 = amplitudes.astype(jnp.bfloat16)
    sent0 = exchange_up(
        transpose_round(amplitudes).reshape(up_count, col_chunk, local_rows)
    )
    up0_cols = up_hop(up_idx, up_table, sent0)
    partial_rows = onsite * amplitudes + down_part(rounded0)
    both = exchange_up(jnp.concatenate([to_columns(partial_rows), up0_cols], axis=1))
    partial_cols = both[:, :col_chunk]
    up0_rows = to_rows(both[:, col_chunk:])
    first_rows = (partial_rows + up0_rows) / half_span

    up1_cols = up_hop(up_idx, up_table, partial_cols, up0_cols)
    down1_rows = down_part(first_rows.astype(jnp.bfloat16))
    up1_rows = to_rows(exchange_up(up1_cols))
    return 2.0 * ((onsite * first_rows + up1_rows + down1_rows) / half_span) - amplitudes


def solution(mesh):
    placed = (P("up", "down"), P("up", "down"), P(), P(), P(), P(), P(), P())
    return jax.shard_map(
        body, mesh=mesh, in_specs=placed, out_specs=P("up", "down"), check_vma=False
    )
```

```python
import jax
import jax.numpy as jnp
from jax import lax
from jax.experimental import pallas as pl
from jax.experimental.pallas import tpu as pltpu
from jax.sharding import PartitionSpec as P


coupling = 0.5
center = 2.0
half_span = 2.0

LANES = 128


def block_order(block_cols, block_ids, shared_count):
    matched = block_ids[:, :, None] == jnp.arange(shared_count, dtype=jnp.int32)[None, None, :]
    return jnp.sum(jnp.where(matched, block_cols[:, :, None], 0), axis=1)


def _fill_rolled(src_ref, src2_ref):
    pairs = src_ref.shape[0]
    half = src_ref.shape[-1] // 2

    def one(i, carry):
        piece = src_ref[i]
        src2_ref[i] = piece
        src2_ref[pairs + i] = pltpu.roll(piece, half, 1)
        return carry

    lax.fori_loop(0, pairs, one, 0)


def _stage_row(idx_ref, base, src2_ref, stage_ref, row0, rows, shared_count, half):
    for t in range(shared_count // 2):
        even = idx_ref[base + 2 * t]
        odd = idx_ref[base + 2 * t + 1]
        stage_ref[row0:row0 + rows, t * LANES:t * LANES + half] = src2_ref[even, :, 0:half]
        stage_ref[row0:row0 + rows, t * LANES + half:(t + 1) * LANES] = src2_ref[odd, :, half:LANES]


def source_index(order, pairs):
    parity = jnp.arange(order.shape[-1], dtype=jnp.int32) % 2
    return ((order & 1) ^ parity) * pairs + (order >> 1)


def up_kernel(idx_ref, x_ref, w_ref, o_ref, src2_ref, stage_ref):
    pairs, n, _ = x_ref.shape
    block_width = w_ref.shape[1]
    shared_count = w_ref.shape[0] // block_width
    rows_per_chunk = stage_ref.shape[0] // n
    _fill_rolled(x_ref, src2_ref)

    def chunk(g, carry):
        for rr in range(rows_per_chunk):
            r = g * rows_per_chunk + rr
            _stage_row(idx_ref, r * shared_count, src2_ref, stage_ref, rr * n, n,
                       shared_count, block_width)
        res = jnp.dot(stage_ref[...], w_ref[...], preferred_element_type=jnp.float32)
        for rr in range(0, rows_per_chunk, 2):
            i = (g * rows_per_chunk + rr) // 2
            o_ref[i, :, 0:block_width] = res[rr * n:(rr + 1) * n]
            o_ref[i, :, block_width:2 * block_width] = res[(rr + 1) * n:(rr + 2) * n]
        return carry

    lax.fori_loop(0, 2 * pairs // rows_per_chunk, chunk, 0)


def down_kernel(idx_ref, g_ref, w_ref, o_ref, src_ref, w2_ref, stage_ref, mask_ref):
    sources, rows, cols = g_ref.shape
    block_width = w_ref.shape[1]
    shared_count = w_ref.shape[0] // block_width
    own_blocks = o_ref.shape[1] // block_width
    per_source = cols // LANES

    def relayout(i, carry):
        for m in range(per_source):
            src_ref[i * per_source + m] = g_ref[i, :, m * LANES:(m + 1) * LANES]
        return carry

    lax.fori_loop(0, sources, relayout, 0)
    for s in range(shared_count):
        block = w_ref[s * block_width:(s + 1) * block_width, :]
        w2_ref[s * LANES:s * LANES + block_width, :] = block
        w2_ref[s * LANES + block_width:(s + 1) * LANES, :] = block
    upper = lax.broadcasted_iota(jnp.int32, (rows, LANES), 1) >= block_width
    ones = jnp.ones((rows, LANES), mask_ref.dtype)
    zeros = jnp.zeros((rows, LANES), mask_ref.dtype)
    mask_ref[0] = jnp.where(upper, zeros, ones)
    mask_ref[1] = jnp.where(upper, ones, zeros)
    for r in range(own_blocks):
        for s in range(shared_count):
            c = idx_ref[r * shared_count + s]
            piece = src_ref[lax.shift_right_logical(c, 1)]
            stage_ref[:, s * LANES:(s + 1) * LANES] = piece * mask_ref[c & 1]
        o_ref[:, r * block_width:(r + 1) * block_width] = jnp.dot(
            stage_ref[...], w2_ref[...], preferred_element_type=jnp.float32
        )


def transpose_round_kernel(x_ref, o_ref):
    for m in range(x_ref.shape[1] // LANES):
        tile = x_ref[:, m * LANES:(m + 1) * LANES]
        o_ref[m * LANES:(m + 1) * LANES, :] = tile.T.astype(o_ref.dtype)


def transpose_round(x):
    rows, cols = x.shape
    return pl.pallas_call(
        transpose_round_kernel,
        out_shape=jax.ShapeDtypeStruct((cols, rows), jnp.bfloat16),
        in_specs=[pl.BlockSpec(memory_space=pltpu.VMEM)],
        out_specs=pl.BlockSpec(memory_space=pltpu.VMEM),
    )(x)


def up_hop(idx, x, w):
    pairs, n, _ = x.shape
    rows_per_chunk = 8
    return pl.pallas_call(
        up_kernel,
        out_shape=jax.ShapeDtypeStruct((pairs, n, LANES), jnp.float32),
        in_specs=[
            pl.BlockSpec(memory_space=pltpu.SMEM),
            pl.BlockSpec(memory_space=pltpu.VMEM),
            pl.BlockSpec(memory_space=pltpu.VMEM),
        ],
        out_specs=pl.BlockSpec(memory_space=pltpu.VMEM),
        scratch_shapes=[
            pltpu.VMEM((2 * pairs, n, LANES), jnp.bfloat16),
            pltpu.VMEM((rows_per_chunk * n, w.shape[0]), jnp.bfloat16),
        ],
    )(idx, x, w)


def down_hop(idx, g, w, own_cols):
    _, rows, _ = g.shape
    return pl.pallas_call(
        down_kernel,
        out_shape=jax.ShapeDtypeStruct((rows, own_cols), jnp.float32),
        in_specs=[
            pl.BlockSpec(memory_space=pltpu.SMEM),
            pl.BlockSpec(memory_space=pltpu.VMEM),
            pl.BlockSpec(memory_space=pltpu.VMEM),
        ],
        out_specs=pl.BlockSpec(memory_space=pltpu.VMEM),
        scratch_shapes=[
            pltpu.VMEM((g.shape[0] * g.shape[2] // LANES, rows, LANES), jnp.bfloat16),
            pltpu.VMEM((2 * w.shape[0], w.shape[1]), jnp.bfloat16),
            pltpu.VMEM((rows, 2 * w.shape[0]), jnp.bfloat16),
            pltpu.VMEM((2, rows, LANES), jnp.bfloat16),
        ],
    )(idx, g, w)


def body(amplitudes, double_occ, up_cols, up_ids, up_blocks, down_cols, down_ids, down_blocks):
    shared_count = up_blocks.shape[0]
    block_width = up_blocks.shape[1]
    local_rows, local_cols = amplitudes.shape
    up_count = lax.axis_size("up")
    own_blocks = local_cols // block_width
    up_idx = source_index(block_order(up_cols, up_ids, shared_count), up_count).reshape(-1)
    down_order = block_order(down_cols, down_ids, shared_count)
    down_idx = lax.dynamic_slice_in_dim(
        down_order, lax.axis_index("down") * own_blocks, own_blocks, 0
    ).reshape(-1)
    up_table = up_blocks.reshape(shared_count * block_width, block_width)
    down_table = down_blocks.reshape(shared_count * block_width, block_width)
    onsite = coupling * double_occ.astype(jnp.float32) - center
    col_chunk = local_cols // up_count

    def to_columns(values):
        return values.T.reshape(up_count, col_chunk, local_rows)

    def to_rows(pieces):
        return pieces.reshape(local_cols, local_rows).T

    def exchange_up(pieces):
        return lax.all_to_all(pieces, "up", 0, 0, tiled=True)

    def down_part(rounded):
        copies = jnp.broadcast_to(rounded[None], (lax.axis_size("down"),) + rounded.shape)
        gathered = lax.all_to_all(copies, "down", 0, 0, tiled=True)
        return down_hop(down_idx, gathered, down_table, local_cols)

    rounded0 = amplitudes.astype(jnp.bfloat16)
    sent0 = exchange_up(
        transpose_round(amplitudes).reshape(up_count, col_chunk, local_rows)
    )
    up0_cols = up_hop(up_idx, sent0, up_table)
    partial_rows = onsite * amplitudes + down_part(rounded0)
    both = exchange_up(jnp.concatenate([to_columns(partial_rows), up0_cols], axis=1))
    partial_cols = both[:, :col_chunk]
    up0_rows = to_rows(both[:, col_chunk:])
    first_cols = (partial_cols + up0_cols) / half_span
    first_rows = (partial_rows + up0_rows) / half_span

    up1_cols = up_hop(up_idx, first_cols.astype(jnp.bfloat16), up_table)
    down1_rows = down_part(first_rows.astype(jnp.bfloat16))
    up1_rows = to_rows(exchange_up(up1_cols))
    return 2.0 * ((onsite * first_rows + up1_rows + down1_rows) / half_span) - amplitudes


def solution(mesh):
    placed = (P("up", "down"), P("up", "down"), P(), P(), P(), P(), P(), P())
    return jax.shard_map(
        body, mesh=mesh, in_specs=placed, out_specs=P("up", "down"), check_vma=False
    )
```
